128 devices in a mesh: rep: 64 (over z, y, x_hi, core), shard: 2 (over x_lo).
Axes of the slice: x: 4 (x_hi: 2, x_lo: 2; x = x_hi * 2 + x_lo), y: 4, z: 4, core: 2. Of those that a mesh axis runs over, the one named last changes fastest.
Arguments:
- grad_xproj: bfloat16 [256, 2, 3072, 128], P(('rep', 'shard')), may hold values from -32 to 32
- grad_chan: bfloat16 [256, 2, 118, 3072], P(('rep', 'shard')), may hold values from -32 to 32
- grad_embed: bfloat16 [256, 1024, 1536], P(('rep', 'shard')), may hold values from -32 to 32
- weight_xproj: float32 [2, 3072, 128], P(None, 'shard'), may hold values from -0.3125 to 0.3125
- weight_chan: float32 [2, 118, 3072], P(None, None, 'shard'), may hold values from -0.3125 to 0.3125
- weight_embed: float32 [1024, 1536], P('shard'), may hold values from -0.3125 to 0.3125
- moment_xproj: float32 [2, 3072, 128], P(None, 'shard'), may hold values from -0.015625 to 0.015625
- moment_chan: float32 [2, 118, 3072], P(None, None, 'shard'), may hold values from -0.015625 to 0.015625
- moment_embed: float32 [1024, 1536], P('shard'), may hold values from -0.015625 to 0.015625
- second_xproj: float32 [2, 3072, 128], P(None, 'shard'), may hold values from 1e-08 to 1e-05
- second_chan: float32 [2, 118, 3072], P(None, None, 'shard'), may hold values from 1e-08 to 1e-05
- second_embed: float32 [1024, 1536], P('shard'), may hold values from 1e-08 to 1e-05
Outputs:
- new_weight_xproj: float32 [2, 3072, 128], P(None, 'shard')
- new_weight_chan: float32 [2, 118, 3072], P(None, None, 'shard')
- new_weight_embed: float32 [1024, 1536], P('shard')
- new_moment_xproj: float32 [2, 3072, 128], P(None, 'shard')
- new_moment_chan: float32 [2, 118, 3072], P(None, None, 'shard')
- new_moment_embed: float32 [1024, 1536], P('shard')
- new_second_xproj: float32 [2, 3072, 128], P(None, 'shard')
- new_second_chan: float32 [2, 118, 3072], P(None, None, 'shard')
- new_second_embed: float32 [1024, 1536], P('shard')
- full_xproj: bfloat16 [2, 3072, 128], replicated
- full_chan: bfloat16 [2, 118, 3072], replicated
- full_embed: bfloat16 [1024, 1536], replicated
- pre_norm: float32 [1], replicated
The draws below stay inside these ranges and needn't reach their ends.
All inputs are finite; a program needn't handle non-finite values.
Results may differ from the reference program's by a relative error of at most 0.00085.
Values may be sent and summed in bfloat16 or wider, within the bound.
No kernel may reach another device: no remote copies, remote signals or barrier semaphores. Data moves between devices by JAX's collectives and lax.ppermute only.
A program may use at most 448 MiB of HBM per device.

```python
import math
import jax
import jax.numpy as jnp
from jax import lax

D = 1536
INNER = 3072
LAYERS = 2
MICRO = 2
EMB_ROWS = 1024
XW = 128
CH = 118
GRADS = 256


def along_dim(vector, dim, rank):
    dims_list = [1] * rank
    dims_list[dim] = vector.shape[0]
    return jnp.reshape(vector, tuple(dims_list))


def gradient_draw(key, full_shape, src_dim, dst_dim):
    rank = len(full_shape)
    devices = GRADS // MICRO
    values = jnp.clip(jax.random.normal(key, full_shape, jnp.float32), -4.5, 4.5)
    ramp_power = 0.5
    pairing = jax.random.permutation(jax.random.fold_in(key, 11), devices).astype(jnp.int32)
    owning = jnp.arange(full_shape[src_dim], dtype=jnp.int32) // MICRO
    target = jnp.take(pairing, owning)
    length = full_shape[dst_dim]
    position = jnp.arange(length, dtype=jnp.int32)
    blocks_at = position // (length // devices)
    spike_scale = jnp.where(along_dim(target, src_dim, rank) == along_dim(blocks_at, dst_dim, rank), 4.0, 1.0)
    ramp_scale = jnp.exp(ramp_power * math.log(3.0) * position.astype(jnp.float32) / length)
    return values * spike_scale * along_dim(ramp_scale, dst_dim, rank)


def draw_grad_xproj(key, part):
    return gradient_draw(jax.random.fold_in(key, 101), (GRADS, LAYERS, INNER, XW), 0, 2).astype(jnp.bfloat16)


def draw_grad_chan(key, part):
    return gradient_draw(jax.random.fold_in(key, 202), (GRADS, LAYERS, CH, INNER), 0, 3).astype(jnp.bfloat16)


def draw_grad_embed(key, part):
    return gradient_draw(jax.random.fold_in(key, 303), (GRADS, EMB_ROWS, D), 0, 1).astype(jnp.bfloat16)


def steps_of(stream_key, extent, cuts, low, top_value):
    factor_of, own = 1.0, jax.random.fold_in(stream_key, 6)
    for dim, parts in cuts:
        heights = jnp.exp(jax.random.uniform(jax.random.fold_in(own, dim), (parts,), jnp.float32, low / len(cuts), top_value / len(cuts)))
        factor_of = factor_of * jnp.repeat(heights, extent[dim] // parts).reshape([-1 if axis == dim else 1 for axis in range(len(extent))])
    return factor_of


def scatter_about(own_key, extent, deviation, reach, split=(), held_as=jnp.bfloat16):
    result = deviation * jax.random.normal(own_key, extent, jnp.float32)
    if split:
        result = result * steps_of(own_key, extent, split, -0.22, 0.18)
    return jnp.clip(result, -reach, reach).astype(held_as)


def setup_inputs(seed: int = 0) -> dict:
    keys = jax.random.split(jax.random.key(seed), 13)
    return {
        "grad_xproj": draw_grad_xproj(jax.random.fold_in(keys[12], 71), 0),
        "grad_chan": draw_grad_chan(jax.random.fold_in(keys[12], 71), 0),
        "grad_embed": draw_grad_embed(jax.random.fold_in(keys[12], 71), 0),
        "weight_xproj": scatter_about(keys[3], (LAYERS, INNER, XW), 0.02, 0.3125, ((1, 2),), jnp.float32),
        "weight_chan": scatter_about(keys[4], (LAYERS, CH, INNER), 0.02, 0.3125, ((2, 2),), jnp.float32),
        "weight_embed": scatter_about(keys[5], (EMB_ROWS, D), 0.02, 0.3125, ((0, 2),), jnp.float32),
        "moment_xproj": scatter_about(keys[6], (LAYERS, INNER, XW), 0.001, 0.015625, ((1, 2),), jnp.float32),
        "moment_chan": scatter_about(keys[7], (LAYERS, CH, INNER), 0.001, 0.015625, ((2, 2),), jnp.float32),
        "moment_embed": scatter_about(keys[8], (EMB_ROWS, D), 0.001, 0.015625, ((0, 2),), jnp.float32),
        "second_xproj": jnp.clip(jnp.exp(math.log(9.999999747378752e-06) - 6.9077553 * jax.random.uniform(keys[9], (LAYERS, INNER, XW), jnp.float32) ** steps_of(keys[9], (LAYERS, INNER, XW), ((1, 2),), -0.2, 0.2)), 9.99999993922529e-09, 9.999999747378752e-06),
        "second_chan": jnp.clip(jnp.exp(math.log(9.999999747378752e-06) - 6.9077553 * jax.random.uniform(keys[10], (LAYERS, CH, INNER), jnp.float32) ** steps_of(keys[10], (LAYERS, CH, INNER), ((2, 2),), -0.2, 0.2)), 9.99999993922529e-09, 9.999999747378752e-06),
        "second_embed": jnp.clip(jnp.exp(math.log(9.999999747378752e-06) - 6.9077553 * jax.random.uniform(keys[11], (EMB_ROWS, D), jnp.float32) ** steps_of(keys[11], (EMB_ROWS, D), ((0, 2),), -0.2, 0.2)), 9.99999993922529e-09, 9.999999747378752e-06),
    }


beta_one = 0.9
beta_two = 0.999
learn_rate = 0.003
decay_rate = 0.1
epsilon = 1e-08
correct_one = 0.9999734386011124
correct_two = 0.09520785288629094

def mean_grad(gradients):
    return lax.optimization_barrier(jnp.sum(gradients, axis=0, dtype=jnp.float32)) / gradients.shape[0]

def adamw_update(weight, moment, second, gradient, clip_factor):
    clipped = clip_factor * gradient
    new_moment = beta_one * moment + (1.0 - beta_one) * clipped
    new_second = beta_two * second + (1.0 - beta_two) * clipped * clipped
    step_size = new_moment / correct_one / (jnp.sqrt(new_second / correct_two) + epsilon)
    new_weight = weight - learn_rate * (step_size + decay_rate * weight)
    return (new_weight, new_moment, new_second)

def reference(grad_xproj, grad_chan, grad_embed, weight_xproj, weight_chan, weight_embed, moment_xproj, moment_chan, moment_embed, second_xproj, second_chan, second_embed):
    mean_x = mean_grad(grad_xproj)
    mean_c = mean_grad(grad_chan)
    mean_e = mean_grad(grad_embed)
    squares = jnp.sum(mean_x * mean_x) + jnp.sum(mean_c * mean_c) + jnp.sum(mean_e * mean_e)
    norm_value = jnp.sqrt(squares)
    clip_factor = jnp.minimum(1.0, 1.0 / (norm_value + 1e-06))
    wx, mx, vx = adamw_update(weight_xproj, moment_xproj, second_xproj, mean_x, clip_factor)
    wc, mc, vc = adamw_update(weight_chan, moment_chan, second_chan, mean_c, clip_factor)
    we, me, ve = adamw_update(weight_embed, moment_embed, second_embed, mean_e, clip_factor)
    return (wx, wc, we, mx, mc, me, vx, vc, ve, wx.astype(jnp.bfloat16), wc.astype(jnp.bfloat16), we.astype(jnp.bfloat16), jnp.reshape(norm_value, (1,)))
```

```python
import jax
import jax.numpy as jnp
from jax import lax
from jax.sharding import PartitionSpec as P

beta_one = 0.9
beta_two = 0.999
learn_rate = 0.003
decay_rate = 0.1
epsilon = 1e-08
correct_one = 0.9999734386011124
correct_two = 0.09520785288629094


def adamw_update(weight, moment, second, gradient, clip_factor):
    clipped = clip_factor * gradient
    new_moment = beta_one * moment + (1.0 - beta_one) * clipped
    new_second = beta_two * second + (1.0 - beta_two) * clipped * clipped
    step_size = new_moment / correct_one / (jnp.sqrt(new_second / correct_two) + epsilon)
    new_weight = weight - learn_rate * (step_size + decay_rate * weight)
    return (new_weight, new_moment, new_second)


def on_device(
    grad_xproj,
    grad_chan,
    grad_embed,
    weight_xproj,
    weight_chan,
    weight_embed,
    moment_xproj,
    moment_chan,
    moment_embed,
    second_xproj,
    second_chan,
    second_embed,
):
    count_rep = lax.axis_size("rep")
    count_shard = lax.axis_size("shard")
    micro, layers, inner, xw = grad_xproj.shape
    _, _, ch, _ = grad_chan.shape
    gx = grad_xproj.reshape(micro, layers, count_shard, inner // count_shard, xw)
    summed_x = jnp.transpose(jnp.sum(gx, axis=0, dtype=jnp.float32), (1, 0, 2, 3))
    gc = grad_chan.reshape(micro, layers, ch, count_shard, inner // count_shard)
    summed_c = jnp.transpose(jnp.sum(gc, axis=0, dtype=jnp.float32), (2, 0, 1, 3))
    summed_e = jnp.sum(grad_embed, axis=0, dtype=jnp.float32)
    part_x = lax.psum_scatter(summed_x.astype(jnp.bfloat16), "shard", scatter_dimension=0, tiled=True)
    part_c = lax.psum_scatter(summed_c.astype(jnp.bfloat16), "shard", scatter_dimension=0, tiled=True)
    part_e = lax.psum_scatter(summed_e.astype(jnp.bfloat16), "shard", scatter_dimension=0, tiled=True)
    block_x = lax.psum(part_x, "rep")[0]
    block_c = lax.psum(part_c, "rep")[0]
    block_e = lax.psum(part_e, "rep")
    inverse = 1.0 / (micro * count_rep * count_shard)
    mean_x = block_x.astype(jnp.float32) * inverse
    mean_c = block_c.astype(jnp.float32) * inverse
    mean_e = block_e.astype(jnp.float32) * inverse
    partial_squares = jnp.sum(mean_x * mean_x) + jnp.sum(mean_c * mean_c) + jnp.sum(mean_e * mean_e)
    squares = lax.psum(partial_squares, "shard")
    norm_value = jnp.sqrt(squares)
    clip_factor = jnp.minimum(1.0, 1.0 / (norm_value + 1e-06))
    wx, mx, vx = adamw_update(weight_xproj, moment_xproj, second_xproj, mean_x, clip_factor)
    wc, mc, vc = adamw_update(weight_chan, moment_chan, second_chan, mean_c, clip_factor)
    we, me, ve = adamw_update(weight_embed, moment_embed, second_embed, mean_e, clip_factor)
    gathered = (
        lax.all_gather(wx.astype(jnp.bfloat16), "shard", axis=1, tiled=True),
        lax.all_gather(wc.astype(jnp.bfloat16), "shard", axis=2, tiled=True),
        lax.all_gather(we.astype(jnp.bfloat16), "shard", axis=0, tiled=True),
    )
    return (
        wx,
        wc,
        we,
        mx,
        mc,
        me,
        vx,
        vc,
        ve,
        gathered[0],
        gathered[1],
        gathered[2],
        jnp.reshape(norm_value, (1,)),
    )


def solution(mesh):
    placed = (
        P(("rep", "shard"), None, None, None),
        P(("rep", "shard"), None, None, None),
        P(("rep", "shard"), None, None),
        P(None, "shard", None),
        P(None, None, "shard"),
        P("shard", None),
        P(None, "shard", None),
        P(None, None, "shard"),
        P("shard", None),
        P(None, "shard", None),
        P(None, None, "shard"),
        P("shard", None),
    )
    return jax.shard_map(
        on_device,
        mesh=mesh,
        in_specs=placed,
        out_specs=(
            P(None, "shard", None),
            P(None, None, "shard"),
            P("shard", None),
            P(None, "shard", None),
            P(None, None, "shard"),
            P("shard", None),
            P(None, "shard", None),
            P(None, None, "shard"),
            P("shard", None),
            P(),
            P(),
            P(),
            P(),
        ),
        check_vma=False,
    )
```

```python
import jax
import jax.numpy as jnp
from jax import lax
from jax.sharding import Mesh, PartitionSpec as P

beta_one = 0.9
beta_two = 0.999
learn_rate = 0.003
decay_rate = 0.1
epsilon = 1e-08
correct_one = 0.9999734386011124
correct_two = 0.09520785288629094

AXES = ("z", "y", "xh", "core", "shard")
XRING = ("xh", "shard")


def adamw_update(weight, moment, second, gradient, clip_factor):
    clipped = clip_factor * gradient
    new_moment = beta_one * moment + (1.0 - beta_one) * clipped
    new_second = beta_two * second + (1.0 - beta_two) * clipped * clipped
    step_size = new_moment / correct_one / (jnp.sqrt(new_second / correct_two) + epsilon)
    new_weight = weight - learn_rate * (step_size + decay_rate * weight)
    return (new_weight, new_moment, new_second)


def reduce_block(buf):
    part = lax.psum_scatter(buf.astype(jnp.bfloat16), "core", scatter_dimension=0, tiled=True)
    part = lax.psum_scatter(part, XRING, scatter_dimension=1, tiled=True)
    part = lax.psum_scatter(part.astype(jnp.float32), "y", scatter_dimension=2, tiled=True)
    part = lax.psum(part, "z").astype(jnp.bfloat16)
    part = lax.all_gather(part, "y", axis=2, tiled=True)
    part = lax.all_gather(part, "xh", axis=1, tiled=True)
    return lax.all_gather(part, "core", axis=0, tiled=True)


def swap_halves(own, split_axis):
    n = lax.axis_size(XRING)
    first, second = jnp.split(own, 2, axis=split_axis)
    from_left = lax.ppermute(first, XRING, perm=[(p, (p + 1) % n) for p in range(n)])
    from_right = lax.ppermute(second, XRING, perm=[(p, (p - 1) % n) for p in range(n)])
    return jnp.concatenate([from_left, from_right], axis=split_axis)


def place(own, other, axis):
    low = lax.axis_index("shard") == 0
    lo = jnp.where(low, own, other)
    hi = jnp.where(low, other, own)
    return jnp.concatenate([lo, hi], axis=axis)


def on_device(
    grad_xproj,
    grad_chan,
    grad_embed,
    weight_xproj,
    weight_chan,
    weight_embed,
    moment_xproj,
    moment_chan,
    moment_embed,
    second_xproj,
    second_chan,
    second_embed,
):
    n_core = lax.axis_size("core")
    n_xh = lax.axis_size("xh")
    n_y = lax.axis_size("y")
    n_s = lax.axis_size("shard")
    total = grad_xproj.shape[0] * lax.axis_size(AXES)
    layers, inner, xw = grad_xproj.shape[1:]
    ch = grad_chan.shape[2]
    rows_e, width = grad_embed.shape[1:]
    half = inner // n_s

    sx = jnp.sum(grad_xproj, axis=0, dtype=jnp.float32)
    sx = sx.reshape(layers, n_s, n_xh, n_y, half // (n_xh * n_y), xw)
    sx = jnp.transpose(sx, (0, 2, 1, 3, 4, 5)).reshape(layers, n_xh * n_s, n_y, half // (n_xh * n_y), xw)

    se = jnp.sum(grad_embed, axis=0, dtype=jnp.float32)
    re = rows_e // (n_s * n_core * n_xh * n_y)
    se = se.reshape(n_s, n_core, n_xh, n_y, re, width)
    se = jnp.transpose(se, (1, 2, 0, 3, 4, 5)).reshape(n_core, n_xh * n_s, n_y, re, width)

    sc = jnp.sum(grad_chan, axis=0, dtype=jnp.float32)
    step = n_xh * n_y * 8
    ch_pad = -(-ch // step) * step
    sc = jnp.pad(sc, ((0, 0), (0, ch_pad - ch), (0, 0)))
    rc = ch_pad // (n_xh * n_y)
    sc = sc.reshape(layers, n_xh, n_y, rc, n_s, half)
    sc = jnp.transpose(sc, (0, 1, 4, 2, 3, 5)).reshape(layers, n_xh * n_s, n_y, rc, half)

    inverse = 1.0 / total
    mean_x = reduce_block(sx).reshape(layers, half, xw).astype(jnp.float32) * inverse
    mean_c = reduce_block(sc).reshape(layers, ch_pad, half)[:, :ch, :].astype(jnp.float32) * inverse
    mean_e = reduce_block(se).reshape(rows_e // n_s, width).astype(jnp.float32) * inverse

    partial_squares = jnp.sum(mean_x * mean_x) + jnp.sum(mean_c * mean_c) + jnp.sum(mean_e * mean_e)
    squares = lax.psum(partial_squares, "shard")
    norm_value = jnp.sqrt(squares)
    clip_factor = jnp.minimum(1.0, 1.0 / (norm_value + 1e-06))
    wx, mx, vx = adamw_update(weight_xproj, moment_xproj, second_xproj, mean_x, clip_factor)
    wc, mc, vc = adamw_update(weight_chan, moment_chan, second_chan, mean_c, clip_factor)
    we, me, ve = adamw_update(weight_embed, moment_embed, second_embed, mean_e, clip_factor)
    bx = wx.astype(jnp.bfloat16)
    bc = wc.astype(jnp.bfloat16)
    be = we.astype(jnp.bfloat16)
    full_x = place(bx, swap_halves(bx, 0), 1)
    full_c = place(bc, swap_halves(bc, 0), 2)
    full_e = place(be, swap_halves(be, 0), 0)
    return (wx, wc, we, mx, mc, me, vx, vc, ve, full_x, full_c, full_e, jnp.reshape(norm_value, (1,)))


def solution(mesh):
    rep = mesh.shape["rep"]
    fine = Mesh(mesh.devices.reshape(rep // 16, 4, 2, 2, mesh.shape["shard"]), AXES)
    grads = ("z", "y", "xh", "core", "shard")
    placed = (
        P(grads, None, None, None),
        P(grads, None, None, None),
        P(grads, None, None),
        P(None, "shard", None),
        P(None, None, "shard"),
        P("shard", None),
        P(None, "shard", None),
        P(None, None, "shard"),
        P("shard", None),
        P(None, "shard", None),
        P(None, None, "shard"),
        P("shard", None),
    )
    return jax.shard_map(
        on_device,
        mesh=fine,
        in_specs=placed,
        out_specs=(
            P(None, "shard", None),
            P(None, None, "shard"),
            P("shard", None),
            P(None, "shard", None),
            P(None, None, "shard"),
            P("shard", None),
            P(None, "shard", None),
            P(None, None, "shard"),
            P("shard", None),
            P(),
            P(),
            P(),
            P(),
        ),
        check_vma=False,
    )
```

```python
import jax
import jax.numpy as jnp
from jax import lax
from jax.sharding import Mesh, PartitionSpec as P

beta_one = 0.9
beta_two = 0.999
learn_rate = 0.003
decay_rate = 0.1
epsilon = 1e-08
correct_one = 0.9999734386011124
correct_two = 0.09520785288629094

AXES = ("z", "y", "xh", "core", "shard")
XRING = ("xh", "shard")


def adamw_update(weight, moment, second, gradient, clip_factor):
    clipped = clip_factor * gradient
    new_moment = beta_one * moment + (1.0 - beta_one) * clipped
    new_second = beta_two * second + (1.0 - beta_two) * clipped * clipped
    step_size = new_moment / correct_one / (jnp.sqrt(new_second / correct_two) + epsilon)
    new_weight = weight - learn_rate * (step_size + decay_rate * weight)
    return (new_weight, new_moment, new_second)


def reduce_flat(buf):
    part = lax.psum_scatter(buf.astype(jnp.bfloat16), "core", scatter_dimension=0, tiled=False)
    part = lax.psum_scatter(part, XRING, scatter_dimension=0, tiled=False)
    part = lax.psum_scatter(part.astype(jnp.float32), "y", scatter_dimension=0, tiled=False)
    part = lax.psum(part, "z").astype(jnp.bfloat16)
    part = lax.all_gather(part, "y", axis=0)
    part = lax.all_gather(part, "xh", axis=0)
    return lax.all_gather(part, "core", axis=0)


def to_tiles(a):
    *lead, r, c = a.shape
    a = a.reshape(*lead, r // 8, 8, c // 128, 128)
    n = len(lead)
    return jnp.swapaxes(a, n + 1, n + 2)


def from_tiles(t, r, c):
    *lead, _, _, _, _ = t.shape
    n = len(lead)
    return jnp.swapaxes(t, n + 1, n + 2).reshape(*lead, r, c)


def swap_halves(own, split_axis):
    n = lax.axis_size(XRING)
    first, second = jnp.split(own, 2, axis=split_axis)
    from_left = lax.ppermute(first, XRING, perm=[(p, (p + 1) % n) for p in range(n)])
    from_right = lax.ppermute(second, XRING, perm=[(p, (p - 1) % n) for p in range(n)])
    return jnp.concatenate([from_left, from_right], axis=split_axis)


def place(own, other, axis):
    low = lax.axis_index("shard") == 0
    lo = jnp.where(low, own, other)
    hi = jnp.where(low, other, own)
    return jnp.concatenate([lo, hi], axis=axis)


def on_device(
    grad_xproj,
    grad_chan,
    grad_embed,
    weight_xproj,
    weight_chan,
    weight_embed,
    moment_xproj,
    moment_chan,
    moment_embed,
    second_xproj,
    second_chan,
    second_embed,
):
    n_core = lax.axis_size("core")
    n_xh = lax.axis_size("xh")
    n_y = lax.axis_size("y")
    n_s = lax.axis_size("shard")
    total = grad_xproj.shape[0] * lax.axis_size(AXES)
    layers, inner, xw = grad_xproj.shape[1:]
    ch = grad_chan.shape[2]
    rows_e, width = grad_embed.shape[1:]
    half = inner // n_s

    n_x = n_xh * n_s
    cut = n_core * n_xh * n_y
    sx = to_tiles(jnp.sum(grad_xproj, axis=0, dtype=jnp.float32))
    tx = sx.reshape(layers, n_s, inner // (8 * n_s), 8, 128)
    tx = jnp.transpose(tx, (1, 0, 2, 3, 4)).reshape(n_s, -1, 8, 128)

    ch_pad = -(-ch // 8) * 8
    sc = jnp.sum(grad_chan, axis=0, dtype=jnp.float32)
    sc = to_tiles(jnp.pad(sc, ((0, 0), (0, ch_pad - ch), (0, 0))))
    lanes_c = half // 128
    tc = sc.reshape(layers, ch_pad // 8, n_s, lanes_c, 8, 128)
    tc = jnp.transpose(tc, (2, 0, 1, 3, 4, 5)).reshape(n_s, -1, 8, 128)

    se = to_tiles(jnp.sum(grad_embed, axis=0, dtype=jnp.float32))
    te = se.reshape(n_s, -1, 8, 128)

    counts = (tc.shape[1], tx.shape[1], te.shape[1])
    used = sum(counts)
    per = -(-used // cut)
    pad = jnp.zeros((n_s, per * cut - used, 8, 128), jnp.float32)
    tiles = jnp.concatenate([tc, tx, te, pad], axis=1)
    buf = tiles.reshape(n_s, n_core, n_xh, n_y, per, 8, 128)
    buf = jnp.transpose(buf, (1, 2, 0, 3, 4, 5, 6)).reshape(n_core, n_x, n_y, per, 8, 128)

    mean_t = reduce_flat(buf).reshape(per * cut, 8, 128)
    inverse = 1.0 / total
    mt = mean_t.astype(jnp.float32) * inverse
    gc = mt[: counts[0]].reshape(layers, ch_pad // 8, lanes_c, 8, 128)
    mean_c = from_tiles(gc, ch_pad, half)[:, :ch, :]
    gx = mt[counts[0] : counts[0] + counts[1]].reshape(layers, half // 8, 1, 8, 128)
    mean_x = from_tiles(gx, half, xw)
    ge = mt[counts[0] + counts[1] : used].reshape(rows_e // (8 * n_s), width // 128, 8, 128)
    mean_e = from_tiles(ge, rows_e // n_s, width)

    partial_squares = jnp.sum(mt * mt)
    squares = lax.psum(partial_squares, "shard")
    norm_value = jnp.sqrt(squares)
    clip_factor = jnp.minimum(1.0, 1.0 / (norm_value + 1e-06))
    wx, mx, vx = adamw_update(weight_xproj, moment_xproj, second_xproj, mean_x, clip_factor)
    wc, mc, vc = adamw_update(weight_chan, moment_chan, second_chan, mean_c, clip_factor)
    we, me, ve = adamw_update(weight_embed, moment_embed, second_embed, mean_e, clip_factor)
    bx = wx.astype(jnp.bfloat16)
    bc = wc.astype(jnp.bfloat16)
    be = we.astype(jnp.bfloat16)
    full_x = place(bx, swap_halves(bx, 0), 1)
    full_c = place(bc, swap_halves(bc, 0), 2)
    full_e = place(be, swap_halves(be, 0), 0)
    return (wx, wc, we, mx, mc, me, vx, vc, ve, full_x, full_c, full_e, jnp.reshape(norm_value, (1,)))


def solution(mesh):
    rep = mesh.shape["rep"]
    fine = Mesh(mesh.devices.reshape(rep // 16, 4, 2, 2, mesh.shape["shard"]), AXES)
    grads = ("z", "y", "xh", "core", "shard")
    placed = (
        P(grads, None, None, None),
        P(grads, None, None, None),
        P(grads, None, None),
        P(None, "shard", None),
        P(None, None, "shard"),
        P("shard", None),
        P(None, "shard", None),
        P(None, None, "shard"),
        P("shard", None),
        P(None, "shard", None),
        P(None, None, "shard"),
        P("shard", None),
    )
    return jax.shard_map(
        on_device,
        mesh=fine,
        in_specs=placed,
        out_specs=(
            P(None, "shard", None),
            P(None, None, "shard"),
            P("shard", None),
            P(None, "shard", None),
            P(None, None, "shard"),
            P("shard", None),
            P(None, "shard", None),
            P(None, None, "shard"),
            P("shard", None),
            P(),
            P(),
            P(),
            P(),
        ),
        check_vma=False,
    )
```

```python
import jax
import jax.numpy as jnp
from jax import lax
from jax.sharding import Mesh, PartitionSpec as P

beta_one = 0.9
beta_two = 0.999
learn_rate = 0.003
decay_rate = 0.1
epsilon = 1e-08
correct_one = 0.9999734386011124
correct_two = 0.09520785288629094

AXES = ("z", "y", "xh", "core", "shard")
XRING = ("xh", "shard")


def adamw_update(weight, moment, second, gradient, clip_factor):
    clipped = clip_factor * gradient
    new_moment = beta_one * moment + (1.0 - beta_one) * clipped
    new_second = beta_two * second + (1.0 - beta_two) * clipped * clipped
    step_size = new_moment / correct_one / (jnp.sqrt(new_second / correct_two) + epsilon)
    new_weight = weight - learn_rate * (step_size + decay_rate * weight)
    return (new_weight, new_moment, new_second)


def reduce_flat(buf):
    part = lax.psum_scatter(buf.astype(jnp.bfloat16), "core", scatter_dimension=0, tiled=False)
    part = lax.psum_scatter(part, XRING, scatter_dimension=0, tiled=False)
    part = lax.psum_scatter(part.astype(jnp.float32), "y", scatter_dimension=0, tiled=False)
    part = lax.psum(part, "z").astype(jnp.bfloat16)
    part = lax.all_gather(part, "y", axis=0)
    part = lax.all_gather(part, "xh", axis=0)
    return lax.all_gather(part, "core", axis=0)


def reduce_staged(buf):
    part = lax.psum_scatter(buf.astype(jnp.bfloat16), "core", scatter_dimension=0, tiled=False)
    part = lax.psum_scatter(part, XRING, scatter_dimension=0, tiled=False)
    part = lax.psum_scatter(part.astype(jnp.float32), "y", scatter_dimension=0, tiled=False)
    part = lax.psum_scatter(part, "z", scatter_dimension=0, tiled=False)
    return lax.all_gather(part.astype(jnp.bfloat16), AXES[:-1], axis=0)


def to_tiles(a):
    *lead, r, c = a.shape
    a = a.reshape(*lead, r // 8, 8, c // 128, 128)
    n = len(lead)
    return jnp.swapaxes(a, n + 1, n + 2)


def from_tiles(t, r, c):
    *lead, _, _, _, _ = t.shape
    n = len(lead)
    return jnp.swapaxes(t, n + 1, n + 2).reshape(*lead, r, c)


def swap_halves(own, split_axis):
    n = lax.axis_size(XRING)
    first, second = jnp.split(own, 2, axis=split_axis)
    from_left = lax.ppermute(first, XRING, perm=[(p, (p + 1) % n) for p in range(n)])
    from_right = lax.ppermute(second, XRING, perm=[(p, (p - 1) % n) for p in range(n)])
    return jnp.concatenate([from_left, from_right], axis=split_axis)


def place(own, other, axis):
    low = lax.axis_index("shard") == 0
    lo = jnp.where(low, own, other)
    hi = jnp.where(low, other, own)
    return jnp.concatenate([lo, hi], axis=axis)


def on_device(
    grad_xproj,
    grad_chan,
    grad_embed,
    weight_xproj,
    weight_chan,
    weight_embed,
    moment_xproj,
    moment_chan,
    moment_embed,
    second_xproj,
    second_chan,
    second_embed,
):
    n_core = lax.axis_size("core")
    n_xh = lax.axis_size("xh")
    n_y = lax.axis_size("y")
    n_s = lax.axis_size("shard")
    total = grad_xproj.shape[0] * lax.axis_size(AXES)
    layers, inner, xw = grad_xproj.shape[1:]
    ch = grad_chan.shape[2]
    rows_e, width = grad_embed.shape[1:]
    half = inner // n_s

    n_x = n_xh * n_s
    n_rep = lax.axis_size(AXES[:-1])
    cut = n_rep
    sx = to_tiles(jnp.sum(grad_xproj, axis=0, dtype=jnp.float32))
    tx = sx.reshape(layers, n_s, inner // (8 * n_s), 8, 128)
    tx = jnp.transpose(tx, (1, 0, 2, 3, 4)).reshape(n_s, -1, 8, 128)

    ch_pad = -(-ch // 8) * 8
    sc = jnp.sum(grad_chan, axis=0, dtype=jnp.float32)
    sc = to_tiles(jnp.pad(sc, ((0, 0), (0, ch_pad - ch), (0, 0))))
    lanes_c = half // 128
    tc = sc.reshape(layers, ch_pad // 8, n_s, lanes_c, 8, 128)
    tc = jnp.transpose(tc, (2, 0, 1, 3, 4, 5)).reshape(n_s, -1, 8, 128)

    se = to_tiles(jnp.sum(grad_embed, axis=0, dtype=jnp.float32))
    te = se.reshape(n_s, -1, 8, 128)

    counts = (tc.shape[1], tx.shape[1], te.shape[1])
    used = sum(counts)
    per = -(-used // cut)
    pad = jnp.zeros((n_s, per * cut - used, 8, 128), jnp.float32)
    tiles = jnp.concatenate([tc, tx, te, pad], axis=1)
    n_z = lax.axis_size("z")
    buf = tiles.reshape(n_s, n_z, n_y, n_xh, n_core, per, 8, 128)
    buf = jnp.transpose(buf, (4, 3, 0, 2, 1, 5, 6, 7)).reshape(n_core, n_x, n_y, n_z, per, 8, 128)

    mean_t = reduce_staged(buf).reshape(per * cut, 8, 128)
    inverse = 1.0 / total
    mt = mean_t.astype(jnp.float32) * inverse
    gc = mt[: counts[0]].reshape(layers, ch_pad // 8, lanes_c, 8, 128)
    mean_c = from_tiles(gc, ch_pad, half)[:, :ch, :]
    gx = mt[counts[0] : counts[0] + counts[1]].reshape(layers, half // 8, 1, 8, 128)
    mean_x = from_tiles(gx, half, xw)
    ge = mt[counts[0] + counts[1] : used].reshape(rows_e // (8 * n_s), width // 128, 8, 128)
    mean_e = from_tiles(ge, rows_e // n_s, width)

    partial_squares = jnp.sum(mt * mt)
    squares = lax.psum(partial_squares, "shard")
    norm_value = jnp.sqrt(squares)
    clip_factor = jnp.minimum(1.0, 1.0 / (norm_value + 1e-06))
    wx, mx, vx = adamw_update(weight_xproj, moment_xproj, second_xproj, mean_x, clip_factor)
    wc, mc, vc = adamw_update(weight_chan, moment_chan, second_chan, mean_c, clip_factor)
    we, me, ve = adamw_update(weight_embed, moment_embed, second_embed, mean_e, clip_factor)
    bx = wx.astype(jnp.bfloat16)
    bc = wc.astype(jnp.bfloat16)
    be = we.astype(jnp.bfloat16)
    full_x = place(bx, swap_halves(bx, 0), 1)
    full_c = place(bc, swap_halves(bc, 0), 2)
    full_e = place(be, swap_halves(be, 0), 0)
    return (wx, wc, we, mx, mc, me, vx, vc, ve, full_x, full_c, full_e, jnp.reshape(norm_value, (1,)))


def solution(mesh):
    rep = mesh.shape["rep"]
    fine = Mesh(mesh.devices.reshape(rep // 16, 4, 2, 2, mesh.shape["shard"]), AXES)
    grads = ("z", "y", "xh", "core", "shard")
    placed = (
        P(grads, None, None, None),
        P(grads, None, None, None),
        P(grads, None, None),
        P(None, "shard", None),
        P(None, None, "shard"),
        P("shard", None),
        P(None, "shard", None),
        P(None, None, "shard"),
        P("shard", None),
        P(None, "shard", None),
        P(None, None, "shard"),
        P("shard", None),
    )
    return jax.shard_map(
        on_device,
        mesh=fine,
        in_specs=placed,
        out_specs=(
            P(None, "shard", None),
            P(None, None, "shard"),
            P("shard", None),
            P(None, "shard", None),
            P(None, None, "shard"),
            P("shard", None),
            P(None, "shard", None),
            P(None, None, "shard"),
            P("shard", None),
            P(),
            P(),
            P(),
            P(),
        ),
        check_vma=False,
    )
```

```python
import jax
import jax.numpy as jnp
from jax import lax
from jax.sharding import Mesh, PartitionSpec as P

beta_one = 0.9
beta_two = 0.999
learn_rate = 0.003
decay_rate = 0.1
epsilon = 1e-08
correct_one = 0.9999734386011124
correct_two = 0.09520785288629094

AXES = ("z", "y", "xh", "core", "shard")
XRING = ("xh", "shard")


def adamw_update(weight, moment, second, gradient, clip_factor):
    clipped = clip_factor * gradient
    new_moment = beta_one * moment + (1.0 - beta_one) * clipped
    new_second = beta_two * second + (1.0 - beta_two) * clipped * clipped
    step_size = new_moment / correct_one / (jnp.sqrt(new_second / correct_two) + epsilon)
    new_weight = weight - learn_rate * (step_size + decay_rate * weight)
    return (new_weight, new_moment, new_second)


def reduce_flat(buf):
    part = lax.psum_scatter(buf.astype(jnp.bfloat16), "core", scatter_dimension=0, tiled=False)
    part = lax.psum_scatter(part, XRING, scatter_dimension=0, tiled=False)
    part = lax.psum_scatter(part.astype(jnp.float32), "y", scatter_dimension=0, tiled=False)
    part = lax.psum(part, "z")
    squares = lax.psum(jnp.sum(part * part), ("y", "xh", "core", "shard"))
    part = lax.all_gather(part.astype(jnp.bfloat16), "y", axis=0)
    part = lax.all_gather(part, "xh", axis=0)
    return lax.all_gather(part, "core", axis=0), squares


def micro_sum(g):
    acc = g[0].astype(jnp.float32)
    for k in range(1, g.shape[0]):
        acc = acc + g[k].astype(jnp.float32)
    return acc


def to_tiles(a):
    *lead, r, c = a.shape
    a = a.reshape(*lead, r // 8, 8, c // 128, 128)
    n = len(lead)
    return jnp.swapaxes(a, n + 1, n + 2)


def from_tiles(t, r, c):
    *lead, _, _, _, _ = t.shape
    n = len(lead)
    return jnp.swapaxes(t, n + 1, n + 2).reshape(*lead, r, c)


def swap_halves(own, split_axis):
    n = lax.axis_size(XRING)
    first, second = jnp.split(own, 2, axis=split_axis)
    from_left = lax.ppermute(first, XRING, perm=[(p, (p + 1) % n) for p in range(n)])
    from_right = lax.ppermute(second, XRING, perm=[(p, (p - 1) % n) for p in range(n)])
    return jnp.concatenate([from_left, from_right], axis=split_axis)


def place(own, other, axis):
    low = lax.axis_index("shard") == 0
    lo = jnp.where(low, own, other)
    hi = jnp.where(low, other, own)
    return jnp.concatenate([lo, hi], axis=axis)


def on_device(
    grad_xproj,
    grad_chan,
    grad_embed,
    weight_xproj,
    weight_chan,
    weight_embed,
    moment_xproj,
    moment_chan,
    moment_embed,
    second_xproj,
    second_chan,
    second_embed,
):
    n_core = lax.axis_size("core")
    n_xh = lax.axis_size("xh")
    n_y = lax.axis_size("y")
    n_s = lax.axis_size("shard")
    total = grad_xproj.shape[0] * lax.axis_size(AXES)
    layers, inner, xw = grad_xproj.shape[1:]
    ch = grad_chan.shape[2]
    rows_e, width = grad_embed.shape[1:]
    half = inner // n_s

    n_x = n_xh * n_s
    cut = n_core * n_xh * n_y
    sx = to_tiles(micro_sum(grad_xproj))
    tx = sx.reshape(layers, n_s, inner // (8 * n_s), 8, 128)
    tx = jnp.transpose(tx, (1, 0, 2, 3, 4)).reshape(n_s, -1, 8, 128)

    ch_pad = -(-ch // 8) * 8
    sc = micro_sum(grad_chan)
    sc = to_tiles(jnp.pad(sc, ((0, 0), (0, ch_pad - ch), (0, 0))))
    lanes_c = half // 128
    tc = sc.reshape(layers, ch_pad // 8, n_s, lanes_c, 8, 128)
    tc = jnp.transpose(tc, (2, 0, 1, 3, 4, 5)).reshape(n_s, -1, 8, 128)

    se = to_tiles(micro_sum(grad_embed))
    te = se.reshape(n_s, -1, 8, 128)

    counts = (tc.shape[1], tx.shape[1], te.shape[1])
    used = sum(counts)
    per = -(-used // cut)
    pad = jnp.zeros((n_s, per * cut - used, 8, 128), jnp.float32)
    tiles = jnp.concatenate([tc, tx, te, pad], axis=1)
    buf = tiles.reshape(n_s, n_core, n_xh, n_y, per, 8, 128)
    buf = jnp.transpose(buf, (1, 2, 0, 3, 4, 5, 6)).reshape(n_core, n_x, n_y, per, 8, 128)

    summed_t, sum_squares = reduce_flat(buf)
    mean_t = summed_t.reshape(per * cut, 8, 128)
    inverse = 1.0 / total
    mt = mean_t.astype(jnp.float32) * inverse
    gc = mt[: counts[0]].reshape(layers, ch_pad // 8, lanes_c, 8, 128)
    mean_c = from_tiles(gc, ch_pad, half)[:, :ch, :]
    gx = mt[counts[0] : counts[0] + counts[1]].reshape(layers, half // 8, 1, 8, 128)
    mean_x = from_tiles(gx, half, xw)
    ge = mt[counts[0] + counts[1] : used].reshape(rows_e // (8 * n_s), width // 128, 8, 128)
    mean_e = from_tiles(ge, rows_e // n_s, width)

    squares = sum_squares * (inverse * inverse)
    norm_value = jnp.sqrt(squares)
    clip_factor = jnp.minimum(1.0, 1.0 / (norm_value + 1e-06))
    wx, mx, vx = adamw_update(weight_xproj, moment_xproj, second_xproj, mean_x, clip_factor)
    wc, mc, vc = adamw_update(weight_chan, moment_chan, second_chan, mean_c, clip_factor)
    we, me, ve = adamw_update(weight_embed, moment_embed, second_embed, mean_e, clip_factor)
    bx = wx.astype(jnp.bfloat16)
    bc = wc.astype(jnp.bfloat16)
    be = we.astype(jnp.bfloat16)
    full_x = place(bx, swap_halves(bx, 0), 1)
    full_c = place(bc, swap_halves(bc, 0), 2)
    full_e = place(be, swap_halves(be, 0), 0)
    return (wx, wc, we, mx, mc, me, vx, vc, ve, full_x, full_c, full_e, jnp.reshape(norm_value, (1,)))


def solution(mesh):
    rep = mesh.shape["rep"]
    fine = Mesh(mesh.devices.reshape(rep // 16, 4, 2, 2, mesh.shape["shard"]), AXES)
    grads = ("z", "y", "xh", "core", "shard")
    placed = (
        P(grads, None, None, None),
        P(grads, None, None, None),
        P(grads, None, None),
        P(None, "shard", None),
        P(None, None, "shard"),
        P("shard", None),
        P(None, "shard", None),
        P(None, None, "shard"),
        P("shard", None),
        P(None, "shard", None),
        P(None, None, "shard"),
        P("shard", None),
    )
    return jax.shard_map(
        on_device,
        mesh=fine,
        in_specs=placed,
        out_specs=(
            P(None, "shard", None),
            P(None, None, "shard"),
            P("shard", None),
            P(None, "shard", None),
            P(None, None, "shard"),
            P("shard", None),
            P(None, "shard", None),
            P(None, None, "shard"),
            P("shard", None),
            P(),
            P(),
            P(),
            P(),
        ),
        check_vma=False,
    )
```

```python
import jax
import jax.numpy as jnp
from jax import lax
from jax.sharding import Mesh, PartitionSpec as P

beta_one = 0.9
beta_two = 0.999
learn_rate = 0.003
decay_rate = 0.1
epsilon = 1e-08
correct_one = 0.9999734386011124
correct_two = 0.09520785288629094

AXES = ("z", "y", "xh", "core", "shard")
XRING = ("xh", "shard")


def adamw_update(weight, moment, second, gradient, clip_factor):
    clipped = clip_factor * gradient
    new_moment = beta_one * moment + (1.0 - beta_one) * clipped
    new_second = beta_two * second + (1.0 - beta_two) * clipped * clipped
    step_size = new_moment / correct_one / (jnp.sqrt(new_second / correct_two) + epsilon)
    new_weight = weight - learn_rate * (step_size + decay_rate * weight)
    return (new_weight, new_moment, new_second)


def reduce_flat(buf):
    part = lax.psum_scatter(buf.astype(jnp.bfloat16), "core", scatter_dimension=0, tiled=False)
    part = lax.psum_scatter(part, XRING, scatter_dimension=0, tiled=False)
    part = lax.psum_scatter(part.astype(jnp.float32), "y", scatter_dimension=0, tiled=False)
    part = lax.psum(part, "z").astype(jnp.bfloat16)
    part = lax.all_gather(part, "y", axis=0)
    part = lax.all_gather(part, "xh", axis=0)
    return lax.all_gather(part, "core", axis=0)


TR = 16


def to_tiles(a):
    *lead, r, c = a.shape
    a = a.reshape(*lead, r // TR, TR, c // 128, 128)
    n = len(lead)
    return jnp.swapaxes(a, n + 1, n + 2)


def from_tiles(t, r, c):
    *lead, _, _, _, _ = t.shape
    n = len(lead)
    return jnp.swapaxes(t, n + 1, n + 2).reshape(*lead, r, c)


def swap_halves(own, split_axis):
    n = lax.axis_size(XRING)
    first, second = jnp.split(own, 2, axis=split_axis)
    from_left = lax.ppermute(first, XRING, perm=[(p, (p + 1) % n) for p in range(n)])
    from_right = lax.ppermute(second, XRING, perm=[(p, (p - 1) % n) for p in range(n)])
    return jnp.concatenate([from_left, from_right], axis=split_axis)


def place(own, other, axis):
    low = lax.axis_index("shard") == 0
    lo = jnp.where(low, own, other)
    hi = jnp.where(low, other, own)
    return jnp.concatenate([lo, hi], axis=axis)


def on_device(
    grad_xproj,
    grad_chan,
    grad_embed,
    weight_xproj,
    weight_chan,
    weight_embed,
    moment_xproj,
    moment_chan,
    moment_embed,
    second_xproj,
    second_chan,
    second_embed,
):
    n_core = lax.axis_size("core")
    n_xh = lax.axis_size("xh")
    n_y = lax.axis_size("y")
    n_s = lax.axis_size("shard")
    total = grad_xproj.shape[0] * lax.axis_size(AXES)
    layers, inner, xw = grad_xproj.shape[1:]
    ch = grad_chan.shape[2]
    rows_e, width = grad_embed.shape[1:]
    half = inner // n_s

    n_x = n_xh * n_s
    cut = n_core * n_xh * n_y
    sx = to_tiles(jnp.sum(grad_xproj, axis=0, dtype=jnp.float32))
    tx = sx.reshape(layers, n_s, inner // (TR * n_s), TR, 128)
    tx = jnp.transpose(tx, (1, 0, 2, 3, 4)).reshape(n_s, -1, TR, 128)

    ch_pad = -(-ch // TR) * TR
    sc = jnp.sum(grad_chan, axis=0, dtype=jnp.float32)
    sc = to_tiles(jnp.pad(sc, ((0, 0), (0, ch_pad - ch), (0, 0))))
    lanes_c = half // 128
    tc = sc.reshape(layers, ch_pad // TR, n_s, lanes_c, TR, 128)
    tc = jnp.transpose(tc, (2, 0, 1, 3, 4, 5)).reshape(n_s, -1, TR, 128)

    se = to_tiles(jnp.sum(grad_embed, axis=0, dtype=jnp.float32))
    te = se.reshape(n_s, -1, TR, 128)

    counts = (tc.shape[1], tx.shape[1], te.shape[1])
    used = sum(counts)
    per = -(-used // cut)
    parts = [tc, tx, te]
    if per * cut > used:
        parts.append(jnp.zeros((n_s, per * cut - used, TR, 128), jnp.float32))
    tiles = jnp.concatenate(parts, axis=1)
    buf = tiles.reshape(n_s, n_core, n_xh, n_y, per, TR, 128)
    buf = jnp.transpose(buf, (1, 2, 0, 3, 4, 5, 6)).reshape(n_core, n_x, n_y, per, TR, 128)

    mean_t = reduce_flat(buf).reshape(per * cut, TR, 128)
    inverse = 1.0 / total
    mt = mean_t.astype(jnp.float32) * inverse
    gc = mt[: counts[0]].reshape(layers, ch_pad // TR, lanes_c, TR, 128)
    mean_c = from_tiles(gc, ch_pad, half)[:, :ch, :]
    gx = mt[counts[0] : counts[0] + counts[1]].reshape(layers, half // TR, 1, TR, 128)
    mean_x = from_tiles(gx, half, xw)
    ge = mt[counts[0] + counts[1] : used].reshape(rows_e // (TR * n_s), width // 128, TR, 128)
    mean_e = from_tiles(ge, rows_e // n_s, width)

    partial_squares = jnp.sum(mt * mt)
    squares = lax.psum(partial_squares, "shard")
    norm_value = jnp.sqrt(squares)
    clip_factor = jnp.minimum(1.0, 1.0 / (norm_value + 1e-06))
    wx, mx, vx = adamw_update(weight_xproj, moment_xproj, second_xproj, mean_x, clip_factor)
    wc, mc, vc = adamw_update(weight_chan, moment_chan, second_chan, mean_c, clip_factor)
    we, me, ve = adamw_update(weight_embed, moment_embed, second_embed, mean_e, clip_factor)
    bx = wx.astype(jnp.bfloat16)
    bc = wc.astype(jnp.bfloat16)
    be = we.astype(jnp.bfloat16)
    full_x = place(bx, swap_halves(bx, 0), 1)
    full_c = place(bc, swap_halves(bc, 0), 2)
    full_e = place(be, swap_halves(be, 0), 0)
    return (wx, wc, we, mx, mc, me, vx, vc, ve, full_x, full_c, full_e, jnp.reshape(norm_value, (1,)))


def solution(mesh):
    rep = mesh.shape["rep"]
    fine = Mesh(mesh.devices.reshape(rep // 16, 4, 2, 2, mesh.shape["shard"]), AXES)
    grads = ("z", "y", "xh", "core", "shard")
    placed = (
        P(grads, None, None, None),
        P(grads, None, None, None),
        P(grads, None, None),
        P(None, "shard", None),
        P(None, None, "shard"),
        P("shard", None),
        P(None, "shard", None),
        P(None, None, "shard"),
        P("shard", None),
        P(None, "shard", None),
        P(None, None, "shard"),
        P("shard", None),
    )
    return jax.shard_map(
        on_device,
        mesh=fine,
        in_specs=placed,
        out_specs=(
            P(None, "shard", None),
            P(None, None, "shard"),
            P("shard", None),
            P(None, "shard", None),
            P(None, None, "shard"),
            P("shard", None),
            P(None, "shard", None),
            P(None, None, "shard"),
            P("shard", None),
            P(),
            P(),
            P(),
            P(),
        ),
        check_vma=False,
    )
```

```python
import jax
import jax.numpy as jnp
from jax import lax
from jax.sharding import Mesh, PartitionSpec as P

beta_one = 0.9
beta_two = 0.999
learn_rate = 0.003
decay_rate = 0.1
epsilon = 1e-08
correct_one = 0.9999734386011124
correct_two = 0.09520785288629094

AXES = ("z", "y", "xh", "core", "shard")
XRING = ("xh", "shard")


def adamw_update(weight, moment, second, gradient, clip_factor):
    clipped = clip_factor * gradient
    new_moment = beta_one * moment + (1.0 - beta_one) * clipped
    new_second = beta_two * second + (1.0 - beta_two) * clipped * clipped
    step_size = new_moment / correct_one / (jnp.sqrt(new_second / correct_two) + epsilon)
    new_weight = weight - learn_rate * (step_size + decay_rate * weight)
    return (new_weight, new_moment, new_second)


def reduce_flat(buf):
    part = lax.psum_scatter(buf.astype(jnp.bfloat16), "core", scatter_dimension=0, tiled=False)
    part = lax.psum_scatter(part, XRING, scatter_dimension=0, tiled=False)
    part = lax.psum_scatter(part.astype(jnp.float32), "y", scatter_dimension=0, tiled=False)
    part = lax.psum(part, "z").astype(jnp.bfloat16)
    wide = part.astype(jnp.float32)
    squares = jnp.sum(wide * wide)
    part = lax.all_gather(part, "y", axis=0)
    part = lax.all_gather(part, "xh", axis=0)
    part = lax.all_gather(part, "core", axis=0)
    for axis in ("y", XRING, "core"):
        squares = lax.psum(squares, axis)
    return part, squares


TR = 16


def to_tiles(a):
    *lead, r, c = a.shape
    a = a.reshape(*lead, r // TR, TR, c // 128, 128)
    n = len(lead)
    return jnp.swapaxes(a, n + 1, n + 2)


def from_tiles(t, r, c):
    *lead, _, _, _, _ = t.shape
    n = len(lead)
    return jnp.swapaxes(t, n + 1, n + 2).reshape(*lead, r, c)


def swap_halves(own, split_axis):
    n = lax.axis_size(XRING)
    first, second = jnp.split(own, 2, axis=split_axis)
    from_left = lax.ppermute(first, XRING, perm=[(p, (p + 1) % n) for p in range(n)])
    from_right = lax.ppermute(second, XRING, perm=[(p, (p - 1) % n) for p in range(n)])
    return jnp.concatenate([from_left, from_right], axis=split_axis)


def place(own, other, axis):
    low = lax.axis_index("shard") == 0
    lo = jnp.where(low, own, other)
    hi = jnp.where(low, other, own)
    return jnp.concatenate([lo, hi], axis=axis)


def on_device(
    grad_xproj,
    grad_chan,
    grad_embed,
    weight_xproj,
    weight_chan,
    weight_embed,
    moment_xproj,
    moment_chan,
    moment_embed,
    second_xproj,
    second_chan,
    second_embed,
):
    n_core = lax.axis_size("core")
    n_xh = lax.axis_size("xh")
    n_y = lax.axis_size("y")
    n_s = lax.axis_size("shard")
    total = grad_xproj.shape[0] * lax.axis_size(AXES)
    layers, inner, xw = grad_xproj.shape[1:]
    ch = grad_chan.shape[2]
    rows_e, width = grad_embed.shape[1:]
    half = inner // n_s

    n_x = n_xh * n_s
    cut = n_core * n_xh * n_y
    sx = to_tiles(jnp.sum(grad_xproj, axis=0, dtype=jnp.float32))
    tx = sx.reshape(layers, n_s, inner // (TR * n_s), TR, 128)
    tx = jnp.transpose(tx, (1, 0, 2, 3, 4)).reshape(n_s, -1, TR, 128)

    ch_pad = -(-ch // TR) * TR
    sc = jnp.sum(grad_chan, axis=0, dtype=jnp.float32)
    sc = to_tiles(jnp.pad(sc, ((0, 0), (0, ch_pad - ch), (0, 0))))
    lanes_c = half // 128
    tc = sc.reshape(layers, ch_pad // TR, n_s, lanes_c, TR, 128)
    tc = jnp.transpose(tc, (2, 0, 1, 3, 4, 5)).reshape(n_s, -1, TR, 128)

    se = to_tiles(jnp.sum(grad_embed, axis=0, dtype=jnp.float32))
    te = se.reshape(n_s, -1, TR, 128)

    counts = (tc.shape[1], tx.shape[1], te.shape[1])
    used = sum(counts)
    per = -(-used // cut)
    parts = [tc, tx, te]
    if per * cut > used:
        parts.append(jnp.zeros((n_s, per * cut - used, TR, 128), jnp.float32))
    tiles = jnp.concatenate(parts, axis=1)
    buf = tiles.reshape(n_s, n_core, n_xh, n_y, per, TR, 128)
    buf = jnp.transpose(buf, (1, 2, 0, 3, 4, 5, 6)).reshape(n_core, n_x, n_y, per, TR, 128)

    summed_t, sum_squares = reduce_flat(buf)
    mean_t = summed_t.reshape(per * cut, TR, 128)
    inverse = 1.0 / total
    mt = mean_t.astype(jnp.float32) * inverse
    gc = mt[: counts[0]].reshape(layers, ch_pad // TR, lanes_c, TR, 128)
    mean_c = from_tiles(gc, ch_pad, half)[:, :ch, :]
    gx = mt[counts[0] : counts[0] + counts[1]].reshape(layers, half // TR, 1, TR, 128)
    mean_x = from_tiles(gx, half, xw)
    ge = mt[counts[0] + counts[1] : used].reshape(rows_e // (TR * n_s), width // 128, TR, 128)
    mean_e = from_tiles(ge, rows_e // n_s, width)

    squares = sum_squares * (inverse * inverse)
    norm_value = jnp.sqrt(squares)
    clip_factor = jnp.minimum(1.0, 1.0 / (norm_value + 1e-06))
    wx, mx, vx = adamw_update(weight_xproj, moment_xproj, second_xproj, mean_x, clip_factor)
    wc, mc, vc = adamw_update(weight_chan, moment_chan, second_chan, mean_c, clip_factor)
    we, me, ve = adamw_update(weight_embed, moment_embed, second_embed, mean_e, clip_factor)
    bx = wx.astype(jnp.bfloat16)
    bc = wc.astype(jnp.bfloat16)
    be = we.astype(jnp.bfloat16)
    full_x = place(bx, swap_halves(bx, 0), 1)
    full_c = place(bc, swap_halves(bc, 0), 2)
    full_e = place(be, swap_halves(be, 0), 0)
    return (wx, wc, we, mx, mc, me, vx, vc, ve, full_x, full_c, full_e, jnp.reshape(norm_value, (1,)))


def solution(mesh):
    rep = mesh.shape["rep"]
    fine = Mesh(mesh.devices.reshape(rep // 16, 4, 2, 2, mesh.shape["shard"]), AXES)
    grads = ("z", "y", "xh", "core", "shard")
    placed = (
        P(grads, None, None, None),
        P(grads, None, None, None),
        P(grads, None, None),
        P(None, "shard", None),
        P(None, None, "shard"),
        P("shard", None),
        P(None, "shard", None),
        P(None, None, "shard"),
        P("shard", None),
        P(None, "shard", None),
        P(None, None, "shard"),
        P("shard", None),
    )
    return jax.shard_map(
        on_device,
        mesh=fine,
        in_specs=placed,
        out_specs=(
            P(None, "shard", None),
            P(None, None, "shard"),
            P("shard", None),
            P(None, "shard", None),
            P(None, None, "shard"),
            P("shard", None),
            P(None, "shard", None),
            P(None, None, "shard"),
            P("shard", None),
            P(),
            P(),
            P(),
            P(),
        ),
        check_vma=False,
    )
```

```python
import jax
import jax.numpy as jnp
from jax import lax
from jax.sharding import Mesh, PartitionSpec as P

beta_one = 0.9
beta_two = 0.999
learn_rate = 0.003
decay_rate = 0.1
epsilon = 1e-08
correct_one = 0.9999734386011124
correct_two = 0.09520785288629094

AXES = ("z", "y", "xh", "core", "shard")
XRING = ("xh", "shard")


def adamw_update(weight, moment, second, gradient, clip_factor):
    clipped = clip_factor * gradient
    new_moment = beta_one * moment + (1.0 - beta_one) * clipped
    new_second = beta_two * second + (1.0 - beta_two) * clipped * clipped
    step_size = new_moment / correct_one / (jnp.sqrt(new_second / correct_two) + epsilon)
    new_weight = weight - learn_rate * (step_size + decay_rate * weight)
    return (new_weight, new_moment, new_second)


def reduce_flat(buf):
    part = lax.psum_scatter(buf.astype(jnp.bfloat16), "core", scatter_dimension=0, tiled=False)
    part = lax.psum_scatter(part, XRING, scatter_dimension=0, tiled=False)
    part = lax.psum_scatter(part.astype(jnp.float32), "y", scatter_dimension=0, tiled=False)
    part = lax.psum(part, "z").astype(jnp.bfloat16)
    wide = part.astype(jnp.float32)
    squares = jnp.sum(wide * wide)
    for axis in ("core", XRING, "y"):
        squares = lax.psum(squares, axis)
    part = lax.all_gather(part, "y", axis=0)
    part = lax.all_gather(part, "xh", axis=0)
    part, squares = lax.optimization_barrier((part, squares))
    part = lax.all_gather(part, "core", axis=0)
    return part, squares


TR = 16


def to_tiles(a):
    *lead, r, c = a.shape
    a = a.reshape(*lead, r // TR, TR, c // 128, 128)
    n = len(lead)
    return jnp.swapaxes(a, n + 1, n + 2)


def from_tiles(t, r, c):
    *lead, _, _, _, _ = t.shape
    n = len(lead)
    return jnp.swapaxes(t, n + 1, n + 2).reshape(*lead, r, c)


def swap_halves(own, split_axis):
    n = lax.axis_size(XRING)
    first, second = jnp.split(own, 2, axis=split_axis)
    from_left = lax.ppermute(first, XRING, perm=[(p, (p + 1) % n) for p in range(n)])
    from_right = lax.ppermute(second, XRING, perm=[(p, (p - 1) % n) for p in range(n)])
    return jnp.concatenate([from_left, from_right], axis=split_axis)


def place(own, other, axis):
    low = lax.axis_index("shard") == 0
    lo = jnp.where(low, own, other)
    hi = jnp.where(low, other, own)
    return jnp.concatenate([lo, hi], axis=axis)


def on_device(
    grad_xproj,
    grad_chan,
    grad_embed,
    weight_xproj,
    weight_chan,
    weight_embed,
    moment_xproj,
    moment_chan,
    moment_embed,
    second_xproj,
    second_chan,
    second_embed,
):
    n_core = lax.axis_size("core")
    n_xh = lax.axis_size("xh")
    n_y = lax.axis_size("y")
    n_s = lax.axis_size("shard")
    total = grad_xproj.shape[0] * lax.axis_size(AXES)
    layers, inner, xw = grad_xproj.shape[1:]
    ch = grad_chan.shape[2]
    rows_e, width = grad_embed.shape[1:]
    half = inner // n_s

    n_x = n_xh * n_s
    cut = n_core * n_xh * n_y
    sx = to_tiles(jnp.sum(grad_xproj, axis=0, dtype=jnp.float32))
    tx = sx.reshape(layers, n_s, inner // (TR * n_s), TR, 128)
    tx = jnp.transpose(tx, (1, 0, 2, 3, 4)).reshape(n_s, -1, TR, 128)

    ch_pad = -(-ch // TR) * TR
    sc = jnp.sum(grad_chan, axis=0, dtype=jnp.float32)
    sc = to_tiles(jnp.pad(sc, ((0, 0), (0, ch_pad - ch), (0, 0))))
    lanes_c = half // 128
    tc = sc.reshape(layers, ch_pad // TR, n_s, lanes_c, TR, 128)
    tc = jnp.transpose(tc, (2, 0, 1, 3, 4, 5)).reshape(n_s, -1, TR, 128)

    se = to_tiles(jnp.sum(grad_embed, axis=0, dtype=jnp.float32))
    te = se.reshape(n_s, -1, TR, 128)

    counts = (tc.shape[1], tx.shape[1], te.shape[1])
    used = sum(counts)
    per = -(-used // cut)
    parts = [tc, tx, te]
    if per * cut > used:
        parts.append(jnp.zeros((n_s, per * cut - used, TR, 128), jnp.float32))
    tiles = jnp.concatenate(parts, axis=1)
    buf = tiles.reshape(n_s, n_core, n_xh, n_y, per, TR, 128)
    buf = jnp.transpose(buf, (1, 2, 0, 3, 4, 5, 6)).reshape(n_core, n_x, n_y, per, TR, 128)

    summed_t, sum_squares = reduce_flat(buf)
    mean_t = summed_t.reshape(per * cut, TR, 128)
    inverse = 1.0 / total
    mt = mean_t.astype(jnp.float32) * inverse
    gc = mt[: counts[0]].reshape(layers, ch_pad // TR, lanes_c, TR, 128)
    mean_c = from_tiles(gc, ch_pad, half)[:, :ch, :]
    gx = mt[counts[0] : counts[0] + counts[1]].reshape(layers, half // TR, 1, TR, 128)
    mean_x = from_tiles(gx, half, xw)
    ge = mt[counts[0] + counts[1] : used].reshape(rows_e // (TR * n_s), width // 128, TR, 128)
    mean_e = from_tiles(ge, rows_e // n_s, width)

    squares = sum_squares * (inverse * inverse)
    norm_value = jnp.sqrt(squares)
    clip_factor = jnp.minimum(1.0, 1.0 / (norm_value + 1e-06))
    wx, mx, vx = adamw_update(weight_xproj, moment_xproj, second_xproj, mean_x, clip_factor)
    wc, mc, vc = adamw_update(weight_chan, moment_chan, second_chan, mean_c, clip_factor)
    we, me, ve = adamw_update(weight_embed, moment_embed, second_embed, mean_e, clip_factor)
    bx = wx.astype(jnp.bfloat16)
    bc = wc.astype(jnp.bfloat16)
    be = we.astype(jnp.bfloat16)
    full_x = place(bx, swap_halves(bx, 0), 1)
    full_c = place(bc, swap_halves(bc, 0), 2)
    full_e = place(be, swap_halves(be, 0), 0)
    return (wx, wc, we, mx, mc, me, vx, vc, ve, full_x, full_c, full_e, jnp.reshape(norm_value, (1,)))


def solution(mesh):
    rep = mesh.shape["rep"]
    fine = Mesh(mesh.devices.reshape(rep // 16, 4, 2, 2, mesh.shape["shard"]), AXES)
    grads = ("z", "y", "xh", "core", "shard")
    placed = (
        P(grads, None, None, None),
        P(grads, None, None, None),
        P(grads, None, None),
        P(None, "shard", None),
        P(None, None, "shard"),
        P("shard", None),
        P(None, "shard", None),
        P(None, None, "shard"),
        P("shard", None),
        P(None, "shard", None),
        P(None, None, "shard"),
        P("shard", None),
    )
    return jax.shard_map(
        on_device,
        mesh=fine,
        in_specs=placed,
        out_specs=(
            P(None, "shard", None),
            P(None, None, "shard"),
            P("shard", None),
            P(None, "shard", None),
            P(None, None, "shard"),
            P("shard", None),
            P(None, "shard", None),
            P(None, None, "shard"),
            P("shard", None),
            P(),
            P(),
            P(),
            P(),
        ),
        check_vma=False,
    )
```

```python
import jax
import jax.numpy as jnp
from jax import lax
from jax.sharding import Mesh, PartitionSpec as P

beta_one = 0.9
beta_two = 0.999
learn_rate = 0.003
decay_rate = 0.1
epsilon = 1e-08
correct_one = 0.9999734386011124
correct_two = 0.09520785288629094

AXES = ("z", "y", "xh", "core", "shard")
XRING = ("xh", "shard")


def adamw_update(weight, moment, second, gradient, clip_factor):
    clipped = clip_factor * gradient
    new_moment = beta_one * moment + (1.0 - beta_one) * clipped
    new_second = beta_two * second + (1.0 - beta_two) * clipped * clipped
    step_size = new_moment / correct_one / (jnp.sqrt(new_second / correct_two) + epsilon)
    new_weight = weight - learn_rate * (step_size + decay_rate * weight)
    return (new_weight, new_moment, new_second)


def reduce_flat(buf):
    me = lax.axis_index("core")
    flip = [(0, 1), (1, 0)]
    mine = lax.dynamic_index_in_dim(buf, me, 0, keepdims=False)
    theirs = lax.dynamic_index_in_dim(buf, 1 - me, 0, keepdims=False)
    got = lax.ppermute(theirs.astype(jnp.bfloat16), "core", perm=flip)
    part = (mine + got.astype(jnp.float32)).astype(jnp.bfloat16)
    part = lax.psum_scatter(part, XRING, scatter_dimension=0, tiled=False)
    part = lax.psum_scatter(part.astype(jnp.float32), "y", scatter_dimension=0, tiled=False)
    part = lax.psum(part, "z").astype(jnp.bfloat16)
    wide = part.astype(jnp.float32)
    squares = jnp.sum(wide * wide)
    for axis in ("core", XRING, "y"):
        squares = lax.psum(squares, axis)
    part = lax.all_gather(part, "y", axis=0)
    part = lax.all_gather(part, "xh", axis=0)
    part, squares = lax.optimization_barrier((part, squares))
    other = lax.ppermute(part, "core", perm=flip)
    first = me == 0
    part = jnp.stack([jnp.where(first, part, other), jnp.where(first, other, part)])
    return part, squares


TR = 16


def to_tiles(a):
    *lead, r, c = a.shape
    a = a.reshape(*lead, r // TR, TR, c // 128, 128)
    n = len(lead)
    return jnp.swapaxes(a, n + 1, n + 2)


def from_tiles(t, r, c):
    *lead, _, _, _, _ = t.shape
    n = len(lead)
    return jnp.swapaxes(t, n + 1, n + 2).reshape(*lead, r, c)


def swap_halves(own, split_axis):
    n = lax.axis_size(XRING)
    first, second = jnp.split(own, 2, axis=split_axis)
    from_left = lax.ppermute(first, XRING, perm=[(p, (p + 1) % n) for p in range(n)])
    from_right = lax.ppermute(second, XRING, perm=[(p, (p - 1) % n) for p in range(n)])
    return jnp.concatenate([from_left, from_right], axis=split_axis)


def place(own, other, axis):
    low = lax.axis_index("shard") == 0
    lo = jnp.where(low, own, other)
    hi = jnp.where(low, other, own)
    return jnp.concatenate([lo, hi], axis=axis)


def on_device(
    grad_xproj,
    grad_chan,
    grad_embed,
    weight_xproj,
    weight_chan,
    weight_embed,
    moment_xproj,
    moment_chan,
    moment_embed,
    second_xproj,
    second_chan,
    second_embed,
):
    n_core = lax.axis_size("core")
    n_xh = lax.axis_size("xh")
    n_y = lax.axis_size("y")
    n_s = lax.axis_size("shard")
    total = grad_xproj.shape[0] * lax.axis_size(AXES)
    layers, inner, xw = grad_xproj.shape[1:]
    ch = grad_chan.shape[2]
    rows_e, width = grad_embed.shape[1:]
    half = inner // n_s

    n_x = n_xh * n_s
    cut = n_core * n_xh * n_y
    sx = to_tiles(jnp.sum(grad_xproj, axis=0, dtype=jnp.float32))
    tx = sx.reshape(layers, n_s, inner // (TR * n_s), TR, 128)
    tx = jnp.transpose(tx, (1, 0, 2, 3, 4)).reshape(n_s, -1, TR, 128)

    ch_pad = -(-ch // TR) * TR
    sc = jnp.sum(grad_chan, axis=0, dtype=jnp.float32)
    sc = to_tiles(jnp.pad(sc, ((0, 0), (0, ch_pad - ch), (0, 0))))
    lanes_c = half // 128
    tc = sc.reshape(layers, ch_pad // TR, n_s, lanes_c, TR, 128)
    tc = jnp.transpose(tc, (2, 0, 1, 3, 4, 5)).reshape(n_s, -1, TR, 128)

    se = to_tiles(jnp.sum(grad_embed, axis=0, dtype=jnp.float32))
    te = se.reshape(n_s, -1, TR, 128)

    counts = (tc.shape[1], tx.shape[1], te.shape[1])
    used = sum(counts)
    per = -(-used // cut)
    parts = [tc, tx, te]
    if per * cut > used:
        parts.append(jnp.zeros((n_s, per * cut - used, TR, 128), jnp.float32))
    tiles = jnp.concatenate(parts, axis=1)
    buf = tiles.reshape(n_s, n_core, n_xh, n_y, per, TR, 128)
    buf = jnp.transpose(buf, (1, 2, 0, 3, 4, 5, 6)).reshape(n_core, n_x, n_y, per, TR, 128)

    summed_t, sum_squares = reduce_flat(buf)
    mean_t = summed_t.reshape(per * cut, TR, 128)
    inverse = 1.0 / total
    mt = mean_t.astype(jnp.float32) * inverse
    gc = mt[: counts[0]].reshape(layers, ch_pad // TR, lanes_c, TR, 128)
    mean_c = from_tiles(gc, ch_pad, half)[:, :ch, :]
    gx = mt[counts[0] : counts[0] + counts[1]].reshape(layers, half // TR, 1, TR, 128)
    mean_x = from_tiles(gx, half, xw)
    ge = mt[counts[0] + counts[1] : used].reshape(rows_e // (TR * n_s), width // 128, TR, 128)
    mean_e = from_tiles(ge, rows_e // n_s, width)

    squares = sum_squares * (inverse * inverse)
    norm_value = jnp.sqrt(squares)
    clip_factor = jnp.minimum(1.0, 1.0 / (norm_value + 1e-06))
    wx, mx, vx = adamw_update(weight_xproj, moment_xproj, second_xproj, mean_x, clip_factor)
    wc, mc, vc = adamw_update(weight_chan, moment_chan, second_chan, mean_c, clip_factor)
    we, me, ve = adamw_update(weight_embed, moment_embed, second_embed, mean_e, clip_factor)
    bx = wx.astype(jnp.bfloat16)
    bc = wc.astype(jnp.bfloat16)
    be = we.astype(jnp.bfloat16)
    full_x = place(bx, swap_halves(bx, 0), 1)
    full_c = place(bc, swap_halves(bc, 0), 2)
    full_e = place(be, swap_halves(be, 0), 0)
    return (wx, wc, we, mx, mc, me, vx, vc, ve, full_x, full_c, full_e, jnp.reshape(norm_value, (1,)))


def solution(mesh):
    rep = mesh.shape["rep"]
    fine = Mesh(mesh.devices.reshape(rep // 16, 4, 2, 2, mesh.shape["shard"]), AXES)
    grads = ("z", "y", "xh", "core", "shard")
    placed = (
        P(grads, None, None, None),
        P(grads, None, None, None),
        P(grads, None, None),
        P(None, "shard", None),
        P(None, None, "shard"),
        P("shard", None),
        P(None, "shard", None),
        P(None, None, "shard"),
        P("shard", None),
        P(None, "shard", None),
        P(None, None, "shard"),
        P("shard", None),
    )
    return jax.shard_map(
        on_device,
        mesh=fine,
        in_specs=placed,
        out_specs=(
            P(None, "shard", None),
            P(None, None, "shard"),
            P("shard", None),
            P(None, "shard", None),
            P(None, None, "shard"),
            P("shard", None),
            P(None, "shard", None),
            P(None, None, "shard"),
            P("shard", None),
            P(),
            P(),
            P(),
            P(),
        ),
        check_vma=False,
    )
```

```python
import jax
import jax.numpy as jnp
from jax import lax
from jax.sharding import Mesh, PartitionSpec as P

beta_one = 0.9
beta_two = 0.999
learn_rate = 0.003
decay_rate = 0.1
epsilon = 1e-08
correct_one = 0.9999734386011124
correct_two = 0.09520785288629094

AXES = ("z", "y", "xh", "core", "shard")
XRING = ("xh", "shard")


def adamw_update(weight, moment, second, gradient, clip_factor):
    clipped = clip_factor * gradient
    new_moment = beta_one * moment + (1.0 - beta_one) * clipped
    new_second = beta_two * second + (1.0 - beta_two) * clipped * clipped
    step_size = new_moment / correct_one / (jnp.sqrt(new_second / correct_two) + epsilon)
    new_weight = weight - learn_rate * (step_size + decay_rate * weight)
    return (new_weight, new_moment, new_second)


def reduce_flat(buf):
    me = lax.axis_index("core")
    flip = [(0, 1), (1, 0)]
    low = buf.astype(jnp.bfloat16)
    mine = lax.dynamic_index_in_dim(low, me, 0, keepdims=False)
    theirs = lax.dynamic_index_in_dim(low, 1 - me, 0, keepdims=False)
    got = lax.ppermute(theirs, "core", perm=flip)
    part = (mine.astype(jnp.float32) + got.astype(jnp.float32)).astype(jnp.bfloat16)
    part = lax.psum_scatter(part, XRING, scatter_dimension=0, tiled=False)
    part = lax.psum_scatter(part.astype(jnp.float32), "y", scatter_dimension=0, tiled=False)
    part = lax.psum(part, "z").astype(jnp.bfloat16)
    wide = part.astype(jnp.float32)
    squares = jnp.sum(wide * wide)
    for axis in ("core", XRING, "y"):
        squares = lax.psum(squares, axis)
    part = lax.all_gather(part, "y", axis=0)
    part = lax.all_gather(part, "xh", axis=0)
    part, squares = lax.optimization_barrier((part, squares))
    other = lax.ppermute(part, "core", perm=flip)
    first = me == 0
    part = jnp.stack([jnp.where(first, part, other), jnp.where(first, other, part)])
    return part, squares


TR = 16


def to_tiles(a):
    *lead, r, c = a.shape
    a = a.reshape(*lead, r // TR, TR, c // 128, 128)
    n = len(lead)
    return jnp.swapaxes(a, n + 1, n + 2)


def from_tiles(t, r, c):
    *lead, _, _, _, _ = t.shape
    n = len(lead)
    return jnp.swapaxes(t, n + 1, n + 2).reshape(*lead, r, c)


def swap_halves(own, split_axis):
    n = lax.axis_size(XRING)
    first, second = jnp.split(own, 2, axis=split_axis)
    from_left = lax.ppermute(first, XRING, perm=[(p, (p + 1) % n) for p in range(n)])
    from_right = lax.ppermute(second, XRING, perm=[(p, (p - 1) % n) for p in range(n)])
    return jnp.concatenate([from_left, from_right], axis=split_axis)


def place(own, other, axis):
    low = lax.axis_index("shard") == 0
    lo = jnp.where(low, own, other)
    hi = jnp.where(low, other, own)
    return jnp.concatenate([lo, hi], axis=axis)


def on_device(
    grad_xproj,
    grad_chan,
    grad_embed,
    weight_xproj,
    weight_chan,
    weight_embed,
    moment_xproj,
    moment_chan,
    moment_embed,
    second_xproj,
    second_chan,
    second_embed,
):
    n_core = lax.axis_size("core")
    n_xh = lax.axis_size("xh")
    n_y = lax.axis_size("y")
    n_s = lax.axis_size("shard")
    total = grad_xproj.shape[0] * lax.axis_size(AXES)
    layers, inner, xw = grad_xproj.shape[1:]
    ch = grad_chan.shape[2]
    rows_e, width = grad_embed.shape[1:]
    half = inner // n_s

    n_x = n_xh * n_s
    cut = n_core * n_xh * n_y
    sx = to_tiles(jnp.sum(grad_xproj, axis=0, dtype=jnp.float32))
    tx = sx.reshape(layers, n_s, inner // (TR * n_s), TR, 128)
    tx = jnp.transpose(tx, (1, 0, 2, 3, 4)).reshape(n_s, -1, TR, 128)

    ch_pad = -(-ch // TR) * TR
    sc = jnp.sum(grad_chan, axis=0, dtype=jnp.float32)
    sc = to_tiles(jnp.pad(sc, ((0, 0), (0, ch_pad - ch), (0, 0))))
    lanes_c = half // 128
    tc = sc.reshape(layers, ch_pad // TR, n_s, lanes_c, TR, 128)
    tc = jnp.transpose(tc, (2, 0, 1, 3, 4, 5)).reshape(n_s, -1, TR, 128)

    se = to_tiles(jnp.sum(grad_embed, axis=0, dtype=jnp.float32))
    te = se.reshape(n_s, -1, TR, 128)

    counts = (tc.shape[1], tx.shape[1], te.shape[1])
    used = sum(counts)
    per = -(-used // cut)
    parts = [tc, tx, te]
    if per * cut > used:
        parts.append(jnp.zeros((n_s, per * cut - used, TR, 128), jnp.float32))
    tiles = jnp.concatenate(parts, axis=1)
    buf = tiles.reshape(n_s, n_core, n_xh, n_y, per, TR, 128)
    buf = jnp.transpose(buf, (1, 2, 0, 3, 4, 5, 6)).reshape(n_core, n_x, n_y, per, TR, 128)

    summed_t, sum_squares = reduce_flat(buf)
    mean_t = summed_t.reshape(per * cut, TR, 128)
    inverse = 1.0 / total
    mt = mean_t.astype(jnp.float32) * inverse
    gc = mt[: counts[0]].reshape(layers, ch_pad // TR, lanes_c, TR, 128)
    mean_c = from_tiles(gc, ch_pad, half)[:, :ch, :]
    gx = mt[counts[0] : counts[0] + counts[1]].reshape(layers, half // TR, 1, TR, 128)
    mean_x = from_tiles(gx, half, xw)
    ge = mt[counts[0] + counts[1] : used].reshape(rows_e // (TR * n_s), width // 128, TR, 128)
    mean_e = from_tiles(ge, rows_e // n_s, width)

    squares = sum_squares * (inverse * inverse)
    norm_value = jnp.sqrt(squares)
    clip_factor = jnp.minimum(1.0, 1.0 / (norm_value + 1e-06))
    wx, mx, vx = adamw_update(weight_xproj, moment_xproj, second_xproj, mean_x, clip_factor)
    wc, mc, vc = adamw_update(weight_chan, moment_chan, second_chan, mean_c, clip_factor)
    we, me, ve = adamw_update(weight_embed, moment_embed, second_embed, mean_e, clip_factor)
    bx = wx.astype(jnp.bfloat16)
    bc = wc.astype(jnp.bfloat16)
    be = we.astype(jnp.bfloat16)
    full_x = place(bx, swap_halves(bx, 0), 1)
    full_c = place(bc, swap_halves(bc, 0), 2)
    full_e = place(be, swap_halves(be, 0), 0)
    return (wx, wc, we, mx, mc, me, vx, vc, ve, full_x, full_c, full_e, jnp.reshape(norm_value, (1,)))


def solution(mesh):
    rep = mesh.shape["rep"]
    fine = Mesh(mesh.devices.reshape(rep // 16, 4, 2, 2, mesh.shape["shard"]), AXES)
    grads = ("z", "y", "xh", "core", "shard")
    placed = (
        P(grads, None, None, None),
        P(grads, None, None, None),
        P(grads, None, None),
        P(None, "shard", None),
        P(None, None, "shard"),
        P("shard", None),
        P(None, "shard", None),
        P(None, None, "shard"),
        P("shard", None),
        P(None, "shard", None),
        P(None, None, "shard"),
        P("shard", None),
    )
    return jax.shard_map(
        on_device,
        mesh=fine,
        in_specs=placed,
        out_specs=(
            P(None, "shard", None),
            P(None, None, "shard"),
            P("shard", None),
            P(None, "shard", None),
            P(None, None, "shard"),
            P("shard", None),
            P(None, "shard", None),
            P(None, None, "shard"),
            P("shard", None),
            P(),
            P(),
            P(),
            P(),
        ),
        check_vma=False,
    )
```

```python
import jax
import jax.numpy as jnp
from jax import lax
from jax.sharding import Mesh, PartitionSpec as P

beta_one = 0.9
beta_two = 0.999
learn_rate = 0.003
decay_rate = 0.1
epsilon = 1e-08
correct_one = 0.9999734386011124
correct_two = 0.09520785288629094

AXES = ("z", "y", "xh", "core", "shard")
XRING = ("xh", "shard")


def adamw_update(weight, moment, second, gradient, clip_factor):
    clipped = clip_factor * gradient
    new_moment = beta_one * moment + (1.0 - beta_one) * clipped
    new_second = beta_two * second + (1.0 - beta_two) * clipped * clipped
    step_size = new_moment / correct_one / (jnp.sqrt(new_second / correct_two) + epsilon)
    new_weight = weight - learn_rate * (step_size + decay_rate * weight)
    return (new_weight, new_moment, new_second)


def reduce_flat(buf):
    me = lax.axis_index("core")
    flip = [(0, 1), (1, 0)]
    low = buf.astype(jnp.bfloat16)
    mine = lax.dynamic_index_in_dim(low, me, 0, keepdims=False)
    theirs = lax.dynamic_index_in_dim(low, 1 - me, 0, keepdims=False)
    got = lax.ppermute(theirs, "core", perm=flip)
    part = (mine.astype(jnp.float32) + got.astype(jnp.float32)).astype(jnp.bfloat16)
    part = lax.psum_scatter(part, XRING, scatter_dimension=0, tiled=False)
    part = lax.psum_scatter(part.astype(jnp.float32), "y", scatter_dimension=0, tiled=False)
    part = lax.psum(part, "z").astype(jnp.bfloat16)
    wide = part.astype(jnp.float32)
    squares = jnp.sum(wide * wide)
    for axis in ("core", XRING, "y"):
        squares = lax.psum(squares, axis)
    part = lax.all_gather(part, ("xh", "y"), axis=0)
    part, squares = lax.optimization_barrier((part, squares))
    other = lax.ppermute(part, "core", perm=flip)
    first = me == 0
    part = jnp.stack([jnp.where(first, part, other), jnp.where(first, other, part)])
    return part, squares


TR = 16


def to_tiles(a):
    *lead, r, c = a.shape
    a = a.reshape(*lead, r // TR, TR, c // 128, 128)
    n = len(lead)
    return jnp.swapaxes(a, n + 1, n + 2)


def from_tiles(t, r, c):
    *lead, _, _, _, _ = t.shape
    n = len(lead)
    return jnp.swapaxes(t, n + 1, n + 2).reshape(*lead, r, c)


def swap_halves(own, split_axis):
    n = lax.axis_size(XRING)
    first, second = jnp.split(own, 2, axis=split_axis)
    from_left = lax.ppermute(first, XRING, perm=[(p, (p + 1) % n) for p in range(n)])
    from_right = lax.ppermute(second, XRING, perm=[(p, (p - 1) % n) for p in range(n)])
    return jnp.concatenate([from_left, from_right], axis=split_axis)


def place(own, other, axis):
    low = lax.axis_index("shard") == 0
    lo = jnp.where(low, own, other)
    hi = jnp.where(low, other, own)
    return jnp.concatenate([lo, hi], axis=axis)


def on_device(
    grad_xproj,
    grad_chan,
    grad_embed,
    weight_xproj,
    weight_chan,
    weight_embed,
    moment_xproj,
    moment_chan,
    moment_embed,
    second_xproj,
    second_chan,
    second_embed,
):
    n_core = lax.axis_size("core")
    n_xh = lax.axis_size("xh")
    n_y = lax.axis_size("y")
    n_s = lax.axis_size("shard")
    total = grad_xproj.shape[0] * lax.axis_size(AXES)
    layers, inner, xw = grad_xproj.shape[1:]
    ch = grad_chan.shape[2]
    rows_e, width = grad_embed.shape[1:]
    half = inner // n_s

    n_x = n_xh * n_s
    cut = n_core * n_xh * n_y
    sx = to_tiles(jnp.sum(grad_xproj, axis=0, dtype=jnp.float32))
    tx = sx.reshape(layers, n_s, inner // (TR * n_s), TR, 128)
    tx = jnp.transpose(tx, (1, 0, 2, 3, 4)).reshape(n_s, -1, TR, 128)

    ch_pad = -(-ch // TR) * TR
    sc = jnp.sum(grad_chan, axis=0, dtype=jnp.float32)
    sc = to_tiles(jnp.pad(sc, ((0, 0), (0, ch_pad - ch), (0, 0))))
    lanes_c = half // 128
    tc = sc.reshape(layers, ch_pad // TR, n_s, lanes_c, TR, 128)
    tc = jnp.transpose(tc, (2, 0, 1, 3, 4, 5)).reshape(n_s, -1, TR, 128)

    se = to_tiles(jnp.sum(grad_embed, axis=0, dtype=jnp.float32))
    te = se.reshape(n_s, -1, TR, 128)

    counts = (tc.shape[1], tx.shape[1], te.shape[1])
    used = sum(counts)
    per = -(-used // cut)
    parts = [tc, tx, te]
    if per * cut > used:
        parts.append(jnp.zeros((n_s, per * cut - used, TR, 128), jnp.float32))
    tiles = jnp.concatenate(parts, axis=1)
    buf = tiles.reshape(n_s, n_core, n_xh, n_y, per, TR, 128)
    buf = jnp.transpose(buf, (1, 2, 0, 3, 4, 5, 6)).reshape(n_core, n_x, n_y, per, TR, 128)

    summed_t, sum_squares = reduce_flat(buf)
    mean_t = summed_t.reshape(per * cut, TR, 128)
    inverse = 1.0 / total
    mt = mean_t.astype(jnp.float32) * inverse
    gc = mt[: counts[0]].reshape(layers, ch_pad // TR, lanes_c, TR, 128)
    mean_c = from_tiles(gc, ch_pad, half)[:, :ch, :]
    gx = mt[counts[0] : counts[0] + counts[1]].reshape(layers, half // TR, 1, TR, 128)
    mean_x = from_tiles(gx, half, xw)
    ge = mt[counts[0] + counts[1] : used].reshape(rows_e // (TR * n_s), width // 128, TR, 128)
    mean_e = from_tiles(ge, rows_e // n_s, width)

    squares = sum_squares * (inverse * inverse)
    norm_value = jnp.sqrt(squares)
    clip_factor = jnp.minimum(1.0, 1.0 / (norm_value + 1e-06))
    wx, mx, vx = adamw_update(weight_xproj, moment_xproj, second_xproj, mean_x, clip_factor)
    wc, mc, vc = adamw_update(weight_chan, moment_chan, second_chan, mean_c, clip_factor)
    we, me, ve = adamw_update(weight_embed, moment_embed, second_embed, mean_e, clip_factor)
    bx = wx.astype(jnp.bfloat16)
    bc = wc.astype(jnp.bfloat16)
    be = we.astype(jnp.bfloat16)
    full_x = place(bx, swap_halves(bx, 0), 1)
    full_c = place(bc, swap_halves(bc, 0), 2)
    full_e = place(be, swap_halves(be, 0), 0)
    return (wx, wc, we, mx, mc, me, vx, vc, ve, full_x, full_c, full_e, jnp.reshape(norm_value, (1,)))


def solution(mesh):
    rep = mesh.shape["rep"]
    fine = Mesh(mesh.devices.reshape(rep // 16, 4, 2, 2, mesh.shape["shard"]), AXES)
    grads = ("z", "y", "xh", "core", "shard")
    placed = (
        P(grads, None, None, None),
        P(grads, None, None, None),
        P(grads, None, None),
        P(None, "shard", None),
        P(None, None, "shard"),
        P("shard", None),
        P(None, "shard", None),
        P(None, None, "shard"),
        P("shard", None),
        P(None, "shard", None),
        P(None, None, "shard"),
        P("shard", None),
    )
    return jax.shard_map(
        on_device,
        mesh=fine,
        in_specs=placed,
        out_specs=(
            P(None, "shard", None),
            P(None, None, "shard"),
            P("shard", None),
            P(None, "shard", None),
            P(None, None, "shard"),
            P("shard", None),
            P(None, "shard", None),
            P(None, None, "shard"),
            P("shard", None),
            P(),
            P(),
            P(),
            P(),
        ),
        check_vma=False,
    )
```

```python
import jax
import jax.numpy as jnp
from jax import lax
from jax.sharding import Mesh, PartitionSpec as P

beta_one = 0.9
beta_two = 0.999
learn_rate = 0.003
decay_rate = 0.1
epsilon = 1e-08
correct_one = 0.9999734386011124
correct_two = 0.09520785288629094

AXES = ("z", "y", "xh", "core", "shard")
XRING = ("xh", "shard")


def adamw_update(weight, moment, second, gradient, clip_factor):
    clipped = clip_factor * gradient
    new_moment = beta_one * moment + (1.0 - beta_one) * clipped
    new_second = beta_two * second + (1.0 - beta_two) * clipped * clipped
    step_size = new_moment / correct_one / (jnp.sqrt(new_second / correct_two) + epsilon)
    new_weight = weight - learn_rate * (step_size + decay_rate * weight)
    return (new_weight, new_moment, new_second)


def reduce_flat(buf):
    me = lax.axis_index("core")
    flip = [(0, 1), (1, 0)]
    low = buf.astype(jnp.bfloat16)
    mine = lax.dynamic_index_in_dim(low, me, 0, keepdims=False)
    theirs = lax.dynamic_index_in_dim(low, 1 - me, 0, keepdims=False)
    got = lax.ppermute(theirs, "core", perm=flip)
    part = (mine.astype(jnp.float32) + got.astype(jnp.float32)).astype(jnp.bfloat16)
    part = lax.psum_scatter(part, XRING, scatter_dimension=0, tiled=False)
    part = lax.psum_scatter(part, "y", scatter_dimension=0, tiled=False)
    part = lax.psum(part.astype(jnp.float32), "z").astype(jnp.bfloat16)
    wide = part.astype(jnp.float32)
    squares = jnp.sum(wide * wide)
    for axis in ("core", XRING, "y"):
        squares = lax.psum(squares, axis)
    part = lax.all_gather(part, "y", axis=0)
    part = lax.all_gather(part, "xh", axis=0)
    part, squares = lax.optimization_barrier((part, squares))
    other = lax.ppermute(part, "core", perm=flip)
    first = me == 0
    part = jnp.stack([jnp.where(first, part, other), jnp.where(first, other, part)])
    return part, squares


TR = 16


def to_tiles(a):
    *lead, r, c = a.shape
    a = a.reshape(*lead, r // TR, TR, c // 128, 128)
    n = len(lead)
    return jnp.swapaxes(a, n + 1, n + 2)


def from_tiles(t, r, c):
    *lead, _, _, _, _ = t.shape
    n = len(lead)
    return jnp.swapaxes(t, n + 1, n + 2).reshape(*lead, r, c)


def swap_halves(own, split_axis):
    n = lax.axis_size(XRING)
    first, second = jnp.split(own, 2, axis=split_axis)
    from_left = lax.ppermute(first, XRING, perm=[(p, (p + 1) % n) for p in range(n)])
    from_right = lax.ppermute(second, XRING, perm=[(p, (p - 1) % n) for p in range(n)])
    return jnp.concatenate([from_left, from_right], axis=split_axis)


def place(own, other, axis):
    low = lax.axis_index("shard") == 0
    lo = jnp.where(low, own, other)
    hi = jnp.where(low, other, own)
    return jnp.concatenate([lo, hi], axis=axis)


def on_device(
    grad_xproj,
    grad_chan,
    grad_embed,
    weight_xproj,
    weight_chan,
    weight_embed,
    moment_xproj,
    moment_chan,
    moment_embed,
    second_xproj,
    second_chan,
    second_embed,
):
    n_core = lax.axis_size("core")
    n_xh = lax.axis_size("xh")
    n_y = lax.axis_size("y")
    n_s = lax.axis_size("shard")
    total = grad_xproj.shape[0] * lax.axis_size(AXES)
    layers, inner, xw = grad_xproj.shape[1:]
    ch = grad_chan.shape[2]
    rows_e, width = grad_embed.shape[1:]
    half = inner // n_s

    n_x = n_xh * n_s
    cut = n_core * n_xh * n_y
    sx = to_tiles(jnp.sum(grad_xproj, axis=0, dtype=jnp.float32))
    tx = sx.reshape(layers, n_s, inner // (TR * n_s), TR, 128)
    tx = jnp.transpose(tx, (1, 0, 2, 3, 4)).reshape(n_s, -1, TR, 128)

    ch_pad = -(-ch // TR) * TR
    sc = jnp.sum(grad_chan, axis=0, dtype=jnp.float32)
    sc = to_tiles(jnp.pad(sc, ((0, 0), (0, ch_pad - ch), (0, 0))))
    lanes_c = half // 128
    tc = sc.reshape(layers, ch_pad // TR, n_s, lanes_c, TR, 128)
    tc = jnp.transpose(tc, (2, 0, 1, 3, 4, 5)).reshape(n_s, -1, TR, 128)

    se = to_tiles(jnp.sum(grad_embed, axis=0, dtype=jnp.float32))
    te = se.reshape(n_s, -1, TR, 128)

    counts = (tc.shape[1], tx.shape[1], te.shape[1])
    used = sum(counts)
    per = -(-used // cut)
    parts = [tc, tx, te]
    if per * cut > used:
        parts.append(jnp.zeros((n_s, per * cut - used, TR, 128), jnp.float32))
    tiles = jnp.concatenate(parts, axis=1)
    buf = tiles.reshape(n_s, n_core, n_xh, n_y, per, TR, 128)
    buf = jnp.transpose(buf, (1, 2, 0, 3, 4, 5, 6)).reshape(n_core, n_x, n_y, per, TR, 128)

    summed_t, sum_squares = reduce_flat(buf)
    mean_t = summed_t.reshape(per * cut, TR, 128)
    inverse = 1.0 / total
    mt = mean_t.astype(jnp.float32) * inverse
    gc = mt[: counts[0]].reshape(layers, ch_pad // TR, lanes_c, TR, 128)
    mean_c = from_tiles(gc, ch_pad, half)[:, :ch, :]
    gx = mt[counts[0] : counts[0] + counts[1]].reshape(layers, half // TR, 1, TR, 128)
    mean_x = from_tiles(gx, half, xw)
    ge = mt[counts[0] + counts[1] : used].reshape(rows_e // (TR * n_s), width // 128, TR, 128)
    mean_e = from_tiles(ge, rows_e // n_s, width)

    squares = sum_squares * (inverse * inverse)
    norm_value = jnp.sqrt(squares)
    clip_factor = jnp.minimum(1.0, 1.0 / (norm_value + 1e-06))
    wx, mx, vx = adamw_update(weight_xproj, moment_xproj, second_xproj, mean_x, clip_factor)
    wc, mc, vc = adamw_update(weight_chan, moment_chan, second_chan, mean_c, clip_factor)
    we, me, ve = adamw_update(weight_embed, moment_embed, second_embed, mean_e, clip_factor)
    bx = wx.astype(jnp.bfloat16)
    bc = wc.astype(jnp.bfloat16)
    be = we.astype(jnp.bfloat16)
    full_x = place(bx, swap_halves(bx, 0), 1)
    full_c = place(bc, swap_halves(bc, 0), 2)
    full_e = place(be, swap_halves(be, 0), 0)
    return (wx, wc, we, mx, mc, me, vx, vc, ve, full_x, full_c, full_e, jnp.reshape(norm_value, (1,)))


def solution(mesh):
    rep = mesh.shape["rep"]
    fine = Mesh(mesh.devices.reshape(rep // 16, 4, 2, 2, mesh.shape["shard"]), AXES)
    grads = ("z", "y", "xh", "core", "shard")
    placed = (
        P(grads, None, None, None),
        P(grads, None, None, None),
        P(grads, None, None),
        P(None, "shard", None),
        P(None, None, "shard"),
        P("shard", None),
        P(None, "shard", None),
        P(None, None, "shard"),
        P("shard", None),
        P(None, "shard", None),
        P(None, None, "shard"),
        P("shard", None),
    )
    return jax.shard_map(
        on_device,
        mesh=fine,
        in_specs=placed,
        out_specs=(
            P(None, "shard", None),
            P(None, None, "shard"),
            P("shard", None),
            P(None, "shard", None),
            P(None, None, "shard"),
            P("shard", None),
            P(None, "shard", None),
            P(None, None, "shard"),
            P("shard", None),
            P(),
            P(),
            P(),
            P(),
        ),
        check_vma=False,
    )
```

```python
import jax
import jax.numpy as jnp
from jax import lax
from jax.sharding import Mesh, PartitionSpec as P

beta_one = 0.9
beta_two = 0.999
learn_rate = 0.003
decay_rate = 0.1
epsilon = 1e-08
correct_one = 0.9999734386011124
correct_two = 0.09520785288629094

AXES = ("z", "y", "xh", "core", "shard")
XRING = ("xh", "shard")


def adamw_update(weight, moment, second, gradient, clip_factor):
    clipped = clip_factor * gradient
    new_moment = beta_one * moment + (1.0 - beta_one) * clipped
    new_second = beta_two * second + (1.0 - beta_two) * clipped * clipped
    step_size = new_moment / correct_one / (jnp.sqrt(new_second / correct_two) + epsilon)
    new_weight = weight - learn_rate * (step_size + decay_rate * weight)
    return (new_weight, new_moment, new_second)


def reduce_flat(buf):
    me = lax.axis_index("core")
    flip = [(0, 1), (1, 0)]
    low = buf.astype(jnp.bfloat16)
    mine = lax.dynamic_index_in_dim(low, me, 0, keepdims=False)
    theirs = lax.dynamic_index_in_dim(low, 1 - me, 0, keepdims=False)
    got = lax.ppermute(theirs, "core", perm=flip)
    part = (mine.astype(jnp.float32) + got.astype(jnp.float32)).astype(jnp.bfloat16)
    part = lax.psum_scatter(part, XRING, scatter_dimension=0, tiled=False)
    part = lax.psum_scatter(part, "y", scatter_dimension=0, tiled=False)
    part = lax.psum(part.astype(jnp.float32), "z").astype(jnp.bfloat16)
    wide = part.astype(jnp.float32)
    squares = jnp.sum(wide * wide)
    for axis in ("core", XRING, "y"):
        squares = lax.psum(squares, axis)
    part = lax.all_gather(part, "y", axis=0)
    part = lax.all_gather(part, "xh", axis=0)
    part, squares = lax.optimization_barrier((part, squares))
    other = lax.ppermute(part, "core", perm=flip)
    first = me == 0
    part = jnp.stack([jnp.where(first, part, other), jnp.where(first, other, part)])
    return part, squares


TR = 16


def to_tiles(a):
    *lead, r, c = a.shape
    a = a.reshape(*lead, r // TR, TR, c // 128, 128)
    n = len(lead)
    return jnp.swapaxes(a, n + 1, n + 2)


def from_tiles(t, r, c):
    *lead, _, _, _, _ = t.shape
    n = len(lead)
    return jnp.swapaxes(t, n + 1, n + 2).reshape(*lead, r, c)


def swap_halves(own, split_axis):
    n = lax.axis_size(XRING)
    first, second = jnp.split(own, 2, axis=split_axis)
    from_left = lax.ppermute(first, XRING, perm=[(p, (p + 1) % n) for p in range(n)])
    from_right = lax.ppermute(second, XRING, perm=[(p, (p - 1) % n) for p in range(n)])
    return jnp.concatenate([from_left, from_right], axis=split_axis)


def place(own, other, axis):
    low = lax.axis_index("shard") == 0
    lo = jnp.where(low, own, other)
    hi = jnp.where(low, other, own)
    return jnp.concatenate([lo, hi], axis=axis)


def on_device(
    grad_xproj,
    grad_chan,
    grad_embed,
    weight_xproj,
    weight_chan,
    weight_embed,
    moment_xproj,
    moment_chan,
    moment_embed,
    second_xproj,
    second_chan,
    second_embed,
):
    n_core = lax.axis_size("core")
    n_xh = lax.axis_size("xh")
    n_y = lax.axis_size("y")
    n_s = lax.axis_size("shard")
    total = grad_xproj.shape[0] * lax.axis_size(AXES)
    layers, inner, xw = grad_xproj.shape[1:]
    ch = grad_chan.shape[2]
    rows_e, width = grad_embed.shape[1:]
    half = inner // n_s

    n_x = n_xh * n_s
    cut = n_core * n_xh * n_y
    sx = to_tiles(jnp.sum(grad_xproj, axis=0, dtype=jnp.float32))
    tx = sx.reshape(layers, n_s, inner // (TR * n_s), TR, 128)
    tx = jnp.transpose(tx, (1, 0, 2, 3, 4)).reshape(n_s, -1, TR, 128)

    ch_pad = -(-ch // TR) * TR
    sc = jnp.sum(grad_chan, axis=0, dtype=jnp.float32)
    sc = to_tiles(jnp.pad(sc, ((0, 0), (0, ch_pad - ch), (0, 0))))
    lanes_c = half // 128
    tc = sc.reshape(layers, ch_pad // TR, n_s, lanes_c, TR, 128)
    tc = jnp.transpose(tc, (2, 0, 1, 3, 4, 5)).reshape(n_s, -1, TR, 128)

    se = to_tiles(jnp.sum(grad_embed, axis=0, dtype=jnp.float32))
    te = se.reshape(n_s, -1, TR, 128)

    counts = (tc.shape[1], tx.shape[1], te.shape[1])
    used = sum(counts)
    per = -(-used // cut)
    fits = per * cut == used and counts[0] == counts[1] and counts[2] == 2 * counts[0] and n_core == n_xh == 2
    if fits:
        lead = [a.reshape(n_s, n_y, per, TR, 128) for a in (tc, tx)]
        rest = jnp.swapaxes(te.reshape(n_s, n_xh, n_y, per, TR, 128), 0, 1)
        buf = jnp.stack([jnp.stack(lead), rest]).reshape(n_core, n_x, n_y, per, TR, 128)
    else:
        parts = [tc, tx, te]
        if per * cut > used:
            parts.append(jnp.zeros((n_s, per * cut - used, TR, 128), jnp.float32))
        tiles = jnp.concatenate(parts, axis=1)
        buf = tiles.reshape(n_s, n_core, n_xh, n_y, per, TR, 128)
        buf = jnp.transpose(buf, (1, 2, 0, 3, 4, 5, 6)).reshape(n_core, n_x, n_y, per, TR, 128)

    summed_t, sum_squares = reduce_flat(buf)
    mean_t = summed_t.reshape(per * cut, TR, 128)
    inverse = 1.0 / total
    mt = mean_t.astype(jnp.float32) * inverse
    gc = mt[: counts[0]].reshape(layers, ch_pad // TR, lanes_c, TR, 128)
    mean_c = from_tiles(gc, ch_pad, half)[:, :ch, :]
    gx = mt[counts[0] : counts[0] + counts[1]].reshape(layers, half // TR, 1, TR, 128)
    mean_x = from_tiles(gx, half, xw)
    ge = mt[counts[0] + counts[1] : used].reshape(rows_e // (TR * n_s), width // 128, TR, 128)
    mean_e = from_tiles(ge, rows_e // n_s, width)

    squares = sum_squares * (inverse * inverse)
    norm_value = jnp.sqrt(squares)
    clip_factor = jnp.minimum(1.0, 1.0 / (norm_value + 1e-06))
    wx, mx, vx = adamw_update(weight_xproj, moment_xproj, second_xproj, mean_x, clip_factor)
    wc, mc, vc = adamw_update(weight_chan, moment_chan, second_chan, mean_c, clip_factor)
    we, me, ve = adamw_update(weight_embed, moment_embed, second_embed, mean_e, clip_factor)
    bx = wx.astype(jnp.bfloat16)
    bc = wc.astype(jnp.bfloat16)
    be = we.astype(jnp.bfloat16)
    full_x = place(bx, swap_halves(bx, 0), 1)
    full_c = place(bc, swap_halves(bc, 0), 2)
    full_e = place(be, swap_halves(be, 0), 0)
    return (wx, wc, we, mx, mc, me, vx, vc, ve, full_x, full_c, full_e, jnp.reshape(norm_value, (1,)))


def solution(mesh):
    rep = mesh.shape["rep"]
    fine = Mesh(mesh.devices.reshape(rep // 16, 4, 2, 2, mesh.shape["shard"]), AXES)
    grads = ("z", "y", "xh", "core", "shard")
    placed = (
        P(grads, None, None, None),
        P(grads, None, None, None),
        P(grads, None, None),
        P(None, "shard", None),
        P(None, None, "shard"),
        P("shard", None),
        P(None, "shard", None),
        P(None, None, "shard"),
        P("shard", None),
        P(None, "shard", None),
        P(None, None, "shard"),
        P("shard", None),
    )
    return jax.shard_map(
        on_device,
        mesh=fine,
        in_specs=placed,
        out_specs=(
            P(None, "shard", None),
            P(None, None, "shard"),
            P("shard", None),
            P(None, "shard", None),
            P(None, None, "shard"),
            P("shard", None),
            P(None, "shard", None),
            P(None, None, "shard"),
            P("shard", None),
            P(),
            P(),
            P(),
            P(),
        ),
        check_vma=False,
    )
```

```python
import jax
import jax.numpy as jnp
from jax import lax
from jax.sharding import Mesh, PartitionSpec as P

beta_one = 0.9
beta_two = 0.999
learn_rate = 0.003
decay_rate = 0.1
epsilon = 1e-08
correct_one = 0.9999734386011124
correct_two = 0.09520785288629094

AXES = ("z", "y", "xh", "core", "shard")
XRING = ("xh", "shard")


def adamw_update(weight, moment, second, gradient, clip_factor):
    clipped = clip_factor * gradient
    new_moment = beta_one * moment + (1.0 - beta_one) * clipped
    new_second = beta_two * second + (1.0 - beta_two) * clipped * clipped
    step_size = new_moment / correct_one / (jnp.sqrt(new_second / correct_two) + epsilon)
    new_weight = weight - learn_rate * (step_size + decay_rate * weight)
    return (new_weight, new_moment, new_second)


def reduce_flat(buf):
    me = lax.axis_index("core")
    flip = [(0, 1), (1, 0)]
    low = [b.astype(jnp.bfloat16) for b in buf]
    to_low = lax.ppermute(low[0], "core", perm=[(1, 0)])
    to_high = lax.ppermute(low[1], "core", perm=[(0, 1)])
    first = me == 0
    mine = jnp.where(first, low[0], low[1])
    got = jnp.where(first, to_low, to_high)
    part = (mine.astype(jnp.float32) + got.astype(jnp.float32)).astype(jnp.bfloat16)
    part = lax.psum_scatter(part, XRING, scatter_dimension=0, tiled=False)
    part = lax.psum_scatter(part, "y", scatter_dimension=0, tiled=False)
    part = lax.psum(part.astype(jnp.float32), "z").astype(jnp.bfloat16)
    wide = part.astype(jnp.float32)
    squares = jnp.sum(wide * wide)
    for axis in ("core", XRING, "y"):
        squares = lax.psum(squares, axis)
    part = lax.all_gather(part, "y", axis=0)
    part = lax.all_gather(part, "xh", axis=0)
    part, squares = lax.optimization_barrier((part, squares))
    other = lax.ppermute(part, "core", perm=flip)
    part = jnp.stack([jnp.where(first, part, other), jnp.where(first, other, part)])
    return part, squares


TR = 16


def to_tiles(a):
    *lead, r, c = a.shape
    a = a.reshape(*lead, r // TR, TR, c // 128, 128)
    n = len(lead)
    return jnp.swapaxes(a, n + 1, n + 2)


def from_tiles(t, r, c):
    *lead, _, _, _, _ = t.shape
    n = len(lead)
    return jnp.swapaxes(t, n + 1, n + 2).reshape(*lead, r, c)


def swap_halves(own, split_axis):
    n = lax.axis_size(XRING)
    first, second = jnp.split(own, 2, axis=split_axis)
    from_left = lax.ppermute(first, XRING, perm=[(p, (p + 1) % n) for p in range(n)])
    from_right = lax.ppermute(second, XRING, perm=[(p, (p - 1) % n) for p in range(n)])
    return jnp.concatenate([from_left, from_right], axis=split_axis)


def place(own, other, axis):
    low = lax.axis_index("shard") == 0
    lo = jnp.where(low, own, other)
    hi = jnp.where(low, other, own)
    return jnp.concatenate([lo, hi], axis=axis)


def on_device(
    grad_xproj,
    grad_chan,
    grad_embed,
    weight_xproj,
    weight_chan,
    weight_embed,
    moment_xproj,
    moment_chan,
    moment_embed,
    second_xproj,
    second_chan,
    second_embed,
):
    n_core = lax.axis_size("core")
    n_xh = lax.axis_size("xh")
    n_y = lax.axis_size("y")
    n_s = lax.axis_size("shard")
    total = grad_xproj.shape[0] * lax.axis_size(AXES)
    layers, inner, xw = grad_xproj.shape[1:]
    ch = grad_chan.shape[2]
    rows_e, width = grad_embed.shape[1:]
    half = inner // n_s

    n_x = n_xh * n_s
    cut = n_core * n_xh * n_y
    sx = to_tiles(jnp.sum(grad_xproj, axis=0, dtype=jnp.float32))
    tx = sx.reshape(layers, n_s, inner // (TR * n_s), TR, 128)
    tx = jnp.transpose(tx, (1, 0, 2, 3, 4)).reshape(n_s, -1, TR, 128)

    ch_pad = -(-ch // TR) * TR
    sc = jnp.sum(grad_chan, axis=0, dtype=jnp.float32)
    sc = to_tiles(jnp.pad(sc, ((0, 0), (0, ch_pad - ch), (0, 0))))
    lanes_c = half // 128
    tc = sc.reshape(layers, ch_pad // TR, n_s, lanes_c, TR, 128)
    tc = jnp.transpose(tc, (2, 0, 1, 3, 4, 5)).reshape(n_s, -1, TR, 128)

    se = to_tiles(jnp.sum(grad_embed, axis=0, dtype=jnp.float32))
    te = se.reshape(n_s, -1, TR, 128)

    counts = (tc.shape[1], tx.shape[1], te.shape[1])
    used = sum(counts)
    per = -(-used // cut)
    fits = per * cut == used and counts[0] == counts[1] and counts[2] == 2 * counts[0] and n_core == n_xh == 2
    if fits:
        lead = [a.reshape(n_s, n_y, per, TR, 128) for a in (tc, tx)]
        rest = jnp.swapaxes(te.reshape(n_s, n_xh, n_y, per, TR, 128), 0, 1)
        buf = [jnp.stack(lead).reshape(n_x, n_y, per, TR, 128), rest.reshape(n_x, n_y, per, TR, 128)]
    else:
        parts = [tc, tx, te]
        if per * cut > used:
            parts.append(jnp.zeros((n_s, per * cut - used, TR, 128), jnp.float32))
        tiles = jnp.concatenate(parts, axis=1)
        buf = tiles.reshape(n_s, n_core, n_xh, n_y, per, TR, 128)
        buf = list(jnp.transpose(buf, (1, 2, 0, 3, 4, 5, 6)).reshape(n_core, n_x, n_y, per, TR, 128))

    summed_t, sum_squares = reduce_flat(buf)
    mean_t = summed_t.reshape(per * cut, TR, 128)
    inverse = 1.0 / total
    mt = mean_t.astype(jnp.float32) * inverse
    gc = mt[: counts[0]].reshape(layers, ch_pad // TR, lanes_c, TR, 128)
    mean_c = from_tiles(gc, ch_pad, half)[:, :ch, :]
    gx = mt[counts[0] : counts[0] + counts[1]].reshape(layers, half // TR, 1, TR, 128)
    mean_x = from_tiles(gx, half, xw)
    ge = mt[counts[0] + counts[1] : used].reshape(rows_e // (TR * n_s), width // 128, TR, 128)
    mean_e = from_tiles(ge, rows_e // n_s, width)

    squares = sum_squares * (inverse * inverse)
    norm_value = jnp.sqrt(squares)
    clip_factor = jnp.minimum(1.0, 1.0 / (norm_value + 1e-06))
    wx, mx, vx = adamw_update(weight_xproj, moment_xproj, second_xproj, mean_x, clip_factor)
    wc, mc, vc = adamw_update(weight_chan, moment_chan, second_chan, mean_c, clip_factor)
    we, me, ve = adamw_update(weight_embed, moment_embed, second_embed, mean_e, clip_factor)
    bx = wx.astype(jnp.bfloat16)
    bc = wc.astype(jnp.bfloat16)
    be = we.astype(jnp.bfloat16)
    full_x = place(bx, swap_halves(bx, 0), 1)
    full_c = place(bc, swap_halves(bc, 0), 2)
    full_e = place(be, swap_halves(be, 0), 0)
    return (wx, wc, we, mx, mc, me, vx, vc, ve, full_x, full_c, full_e, jnp.reshape(norm_value, (1,)))


def solution(mesh):
    rep = mesh.shape["rep"]
    fine = Mesh(mesh.devices.reshape(rep // 16, 4, 2, 2, mesh.shape["shard"]), AXES)
    grads = ("z", "y", "xh", "core", "shard")
    placed = (
        P(grads, None, None, None),
        P(grads, None, None, None),
        P(grads, None, None),
        P(None, "shard", None),
        P(None, None, "shard"),
        P("shard", None),
        P(None, "shard", None),
        P(None, None, "shard"),
        P("shard", None),
        P(None, "shard", None),
        P(None, None, "shard"),
        P("shard", None),
    )
    return jax.shard_map(
        on_device,
        mesh=fine,
        in_specs=placed,
        out_specs=(
            P(None, "shard", None),
            P(None, None, "shard"),
            P("shard", None),
            P(None, "shard", None),
            P(None, None, "shard"),
            P("shard", None),
            P(None, "shard", None),
            P(None, None, "shard"),
            P("shard", None),
            P(),
            P(),
            P(),
            P(),
        ),
        check_vma=False,
    )
```

```python
import jax
import jax.numpy as jnp
from jax import lax
from jax.sharding import Mesh, PartitionSpec as P

beta_one = 0.9
beta_two = 0.999
learn_rate = 0.003
decay_rate = 0.1
epsilon = 1e-08
correct_one = 0.9999734386011124
correct_two = 0.09520785288629094

AXES = ("z", "y", "xh", "core", "shard")
XRING = ("xh", "shard")


def adamw_update(weight, moment, second, gradient, clip_factor):
    clipped = clip_factor * gradient
    new_moment = beta_one * moment + (1.0 - beta_one) * clipped
    new_second = beta_two * second + (1.0 - beta_two) * clipped * clipped
    step_size = new_moment / correct_one / (jnp.sqrt(new_second / correct_two) + epsilon)
    new_weight = weight - learn_rate * (step_size + decay_rate * weight)
    return (new_weight, new_moment, new_second)


def reduce_flat(buf):
    me = lax.axis_index("core")
    flip = [(0, 1), (1, 0)]
    low = [b.astype(jnp.bfloat16) for b in buf]
    to_low = lax.ppermute(low[0], "core", perm=[(1, 0)])
    to_high = lax.ppermute(low[1], "core", perm=[(0, 1)])
    first = me == 0
    mine = jnp.where(first, low[0], low[1])
    got = jnp.where(first, to_low, to_high)
    part = (mine.astype(jnp.float32) + got.astype(jnp.float32)).astype(jnp.bfloat16)
    part = lax.psum_scatter(part, XRING, scatter_dimension=0, tiled=False)
    part = lax.psum_scatter(part, "y", scatter_dimension=0, tiled=False)
    part = part.astype(jnp.float32)
    n_z = lax.axis_size("z")
    hop = 1
    while hop < n_z:
        part = part + lax.ppermute(part, "z", perm=[(i, i ^ hop) for i in range(n_z)])
        hop *= 2
    part = part.astype(jnp.bfloat16)
    wide = part.astype(jnp.float32)
    squares = jnp.sum(wide * wide)
    for axis in ("core", XRING, "y"):
        squares = lax.psum(squares, axis)
    part = lax.all_gather(part, "y", axis=0)
    part = lax.all_gather(part, "xh", axis=0)
    part, squares = lax.optimization_barrier((part, squares))
    other = lax.ppermute(part, "core", perm=flip)
    part = jnp.stack([jnp.where(first, part, other), jnp.where(first, other, part)])
    return part, squares


TR = 16


def to_tiles(a):
    *lead, r, c = a.shape
    a = a.reshape(*lead, r // TR, TR, c // 128, 128)
    n = len(lead)
    return jnp.swapaxes(a, n + 1, n + 2)


def from_tiles(t, r, c):
    *lead, _, _, _, _ = t.shape
    n = len(lead)
    return jnp.swapaxes(t, n + 1, n + 2).reshape(*lead, r, c)


def swap_halves(own, split_axis):
    n = lax.axis_size(XRING)
    first, second = jnp.split(own, 2, axis=split_axis)
    from_left = lax.ppermute(first, XRING, perm=[(p, (p + 1) % n) for p in range(n)])
    from_right = lax.ppermute(second, XRING, perm=[(p, (p - 1) % n) for p in range(n)])
    return jnp.concatenate([from_left, from_right], axis=split_axis)


def place(own, other, axis):
    low = lax.axis_index("shard") == 0
    lo = jnp.where(low, own, other)
    hi = jnp.where(low, other, own)
    return jnp.concatenate([lo, hi], axis=axis)


def on_device(
    grad_xproj,
    grad_chan,
    grad_embed,
    weight_xproj,
    weight_chan,
    weight_embed,
    moment_xproj,
    moment_chan,
    moment_embed,
    second_xproj,
    second_chan,
    second_embed,
):
    n_core = lax.axis_size("core")
    n_xh = lax.axis_size("xh")
    n_y = lax.axis_size("y")
    n_s = lax.axis_size("shard")
    total = grad_xproj.shape[0] * lax.axis_size(AXES)
    layers, inner, xw = grad_xproj.shape[1:]
    ch = grad_chan.shape[2]
    rows_e, width = grad_embed.shape[1:]
    half = inner // n_s

    n_x = n_xh * n_s
    cut = n_core * n_xh * n_y
    sx = to_tiles(jnp.sum(grad_xproj, axis=0, dtype=jnp.float32))
    tx = sx.reshape(layers, n_s, inner // (TR * n_s), TR, 128)
    tx = jnp.transpose(tx, (1, 0, 2, 3, 4)).reshape(n_s, -1, TR, 128)

    ch_pad = -(-ch // TR) * TR
    sc = jnp.sum(grad_chan, axis=0, dtype=jnp.float32)
    sc = to_tiles(jnp.pad(sc, ((0, 0), (0, ch_pad - ch), (0, 0))))
    lanes_c = half // 128
    tc = sc.reshape(layers, ch_pad // TR, n_s, lanes_c, TR, 128)
    tc = jnp.transpose(tc, (2, 0, 1, 3, 4, 5)).reshape(n_s, -1, TR, 128)

    se = to_tiles(jnp.sum(grad_embed, axis=0, dtype=jnp.float32))
    te = se.reshape(n_s, -1, TR, 128)

    counts = (tc.shape[1], tx.shape[1], te.shape[1])
    used = sum(counts)
    per = -(-used // cut)
    fits = per * cut == used and counts[0] == counts[1] and counts[2] == 2 * counts[0] and n_core == n_xh == 2
    if fits:
        lead = [a.reshape(n_s, n_y, per, TR, 128) for a in (tc, tx)]
        rest = jnp.swapaxes(te.reshape(n_s, n_xh, n_y, per, TR, 128), 0, 1)
        buf = [jnp.stack(lead).reshape(n_x, n_y, per, TR, 128), rest.reshape(n_x, n_y, per, TR, 128)]
    else:
        parts = [tc, tx, te]
        if per * cut > used:
            parts.append(jnp.zeros((n_s, per * cut - used, TR, 128), jnp.float32))
        tiles = jnp.concatenate(parts, axis=1)
        buf = tiles.reshape(n_s, n_core, n_xh, n_y, per, TR, 128)
        buf = list(jnp.transpose(buf, (1, 2, 0, 3, 4, 5, 6)).reshape(n_core, n_x, n_y, per, TR, 128))

    summed_t, sum_squares = reduce_flat(buf)
    mean_t = summed_t.reshape(per * cut, TR, 128)
    inverse = 1.0 / total
    mt = mean_t.astype(jnp.float32) * inverse
    gc = mt[: counts[0]].reshape(layers, ch_pad // TR, lanes_c, TR, 128)
    mean_c = from_tiles(gc, ch_pad, half)[:, :ch, :]
    gx = mt[counts[0] : counts[0] + counts[1]].reshape(layers, half // TR, 1, TR, 128)
    mean_x = from_tiles(gx, half, xw)
    ge = mt[counts[0] + counts[1] : used].reshape(rows_e // (TR * n_s), width // 128, TR, 128)
    mean_e = from_tiles(ge, rows_e // n_s, width)

    squares = sum_squares * (inverse * inverse)
    norm_value = jnp.sqrt(squares)
    clip_factor = jnp.minimum(1.0, 1.0 / (norm_value + 1e-06))
    wx, mx, vx = adamw_update(weight_xproj, moment_xproj, second_xproj, mean_x, clip_factor)
    wc, mc, vc = adamw_update(weight_chan, moment_chan, second_chan, mean_c, clip_factor)
    we, me, ve = adamw_update(weight_embed, moment_embed, second_embed, mean_e, clip_factor)
    bx = wx.astype(jnp.bfloat16)
    bc = wc.astype(jnp.bfloat16)
    be = we.astype(jnp.bfloat16)
    full_x = place(bx, swap_halves(bx, 0), 1)
    full_c = place(bc, swap_halves(bc, 0), 2)
    full_e = place(be, swap_halves(be, 0), 0)
    return (wx, wc, we, mx, mc, me, vx, vc, ve, full_x, full_c, full_e, jnp.reshape(norm_value, (1,)))


def solution(mesh):
    rep = mesh.shape["rep"]
    fine = Mesh(mesh.devices.reshape(rep // 16, 4, 2, 2, mesh.shape["shard"]), AXES)
    grads = ("z", "y", "xh", "core", "shard")
    placed = (
        P(grads, None, None, None),
        P(grads, None, None, None),
        P(grads, None, None),
        P(None, "shard", None),
        P(None, None, "shard"),
        P("shard", None),
        P(None, "shard", None),
        P(None, None, "shard"),
        P("shard", None),
        P(None, "shard", None),
        P(None, None, "shard"),
        P("shard", None),
    )
    return jax.shard_map(
        on_device,
        mesh=fine,
        in_specs=placed,
        out_specs=(
            P(None, "shard", None),
            P(None, None, "shard"),
            P("shard", None),
            P(None, "shard", None),
            P(None, None, "shard"),
            P("shard", None),
            P(None, "shard", None),
            P(None, None, "shard"),
            P("shard", None),
            P(),
            P(),
            P(),
            P(),
        ),
        check_vma=False,
    )
```

```python
import jax
import jax.numpy as jnp
from jax import lax
from jax.sharding import Mesh, PartitionSpec as P

beta_one = 0.9
beta_two = 0.999
learn_rate = 0.003
decay_rate = 0.1
epsilon = 1e-08
correct_one = 0.9999734386011124
correct_two = 0.09520785288629094

AXES = ("z", "y", "xh", "core", "shard")
XRING = ("xh", "shard")


def adamw_update(weight, moment, second, gradient, clip_factor):
    clipped = clip_factor * gradient
    new_moment = beta_one * moment + (1.0 - beta_one) * clipped
    new_second = beta_two * second + (1.0 - beta_two) * clipped * clipped
    step_size = new_moment / correct_one / (jnp.sqrt(new_second / correct_two) + epsilon)
    new_weight = weight - learn_rate * (step_size + decay_rate * weight)
    return (new_weight, new_moment, new_second)


def reduce_flat(buf):
    me = lax.axis_index("core")
    flip = [(0, 1), (1, 0)]
    low = [b.astype(jnp.bfloat16) for b in buf]
    to_low = lax.ppermute(low[0], "core", perm=[(1, 0)])
    to_high = lax.ppermute(low[1], "core", perm=[(0, 1)])
    first = me == 0
    mine = jnp.where(first, low[0], low[1])
    got = jnp.where(first, to_low, to_high)
    part = (mine.astype(jnp.float32) + got.astype(jnp.float32)).astype(jnp.bfloat16)
    part = lax.psum_scatter(part, XRING, scatter_dimension=0, tiled=False)
    part = lax.psum_scatter(part, "y", scatter_dimension=0, tiled=False)
    part = lax.psum(part.astype(jnp.float32), "z").astype(jnp.bfloat16)
    wide = part.astype(jnp.float32)
    squares = jnp.sum(wide * wide)
    for axis in ("core", XRING, "y"):
        squares = lax.psum(squares, axis)
    part = lax.all_gather(part, "y", axis=0)
    part = lax.all_gather(part, "xh", axis=0)
    part, squares = lax.optimization_barrier((part, squares))
    other = lax.ppermute(part, "core", perm=flip)
    part = jnp.stack([jnp.where(first, part, other), jnp.where(first, other, part)])
    return part, squares


TR = 16


def to_tiles(a):
    *lead, r, c = a.shape
    a = a.reshape(*lead, r // TR, TR, c // 128, 128)
    n = len(lead)
    return jnp.swapaxes(a, n + 1, n + 2)


def from_tiles(t, r, c):
    *lead, _, _, _, _ = t.shape
    n = len(lead)
    return jnp.swapaxes(t, n + 1, n + 2).reshape(*lead, r, c)


def swap_halves(own, split_axis):
    n = lax.axis_size(XRING)
    first, second = jnp.split(own, 2, axis=split_axis)
    from_left = lax.ppermute(first, XRING, perm=[(p, (p + 1) % n) for p in range(n)])
    from_right = lax.ppermute(second, XRING, perm=[(p, (p - 1) % n) for p in range(n)])
    return jnp.concatenate([from_left, from_right], axis=split_axis)


def place(own, other, axis):
    s = lax.axis_index("shard")
    size = own.shape[axis]
    shape = list(own.shape)
    shape[axis] = 2 * size
    full = jnp.zeros(shape, own.dtype)
    full = lax.dynamic_update_slice_in_dim(full, other, (1 - s) * size, axis)
    return lax.dynamic_update_slice_in_dim(full, own, s * size, axis)


def on_device(
    grad_xproj,
    grad_chan,
    grad_embed,
    weight_xproj,
    weight_chan,
    weight_embed,
    moment_xproj,
    moment_chan,
    moment_embed,
    second_xproj,
    second_chan,
    second_embed,
):
    n_core = lax.axis_size("core")
    n_xh = lax.axis_size("xh")
    n_y = lax.axis_size("y")
    n_s = lax.axis_size("shard")
    total = grad_xproj.shape[0] * lax.axis_size(AXES)
    layers, inner, xw = grad_xproj.shape[1:]
    ch = grad_chan.shape[2]
    rows_e, width = grad_embed.shape[1:]
    half = inner // n_s

    n_x = n_xh * n_s
    cut = n_core * n_xh * n_y
    sx = to_tiles(jnp.sum(grad_xproj, axis=0, dtype=jnp.float32))
    tx = sx.reshape(layers, n_s, inner // (TR * n_s), TR, 128)
    tx = jnp.transpose(tx, (1, 0, 2, 3, 4)).reshape(n_s, -1, TR, 128)

    ch_pad = -(-ch // TR) * TR
    sc = jnp.sum(grad_chan, axis=0, dtype=jnp.float32)
    sc = to_tiles(jnp.pad(sc, ((0, 0), (0, ch_pad - ch), (0, 0))))
    lanes_c = half // 128
    tc = sc.reshape(layers, ch_pad // TR, n_s, lanes_c, TR, 128)
    tc = jnp.transpose(tc, (2, 0, 1, 3, 4, 5)).reshape(n_s, -1, TR, 128)

    se = to_tiles(jnp.sum(grad_embed, axis=0, dtype=jnp.float32))
    te = se.reshape(n_s, -1, TR, 128)

    counts = (tc.shape[1], tx.shape[1], te.shape[1])
    used = sum(counts)
    per = -(-used // cut)
    fits = per * cut == used and counts[0] == counts[1] and counts[2] == 2 * counts[0] and n_core == n_xh == 2
    if fits:
        lead = [a.reshape(n_s, n_y, per, TR, 128) for a in (tc, tx)]
        rest = jnp.swapaxes(te.reshape(n_s, n_xh, n_y, per, TR, 128), 0, 1)
        buf = [jnp.stack(lead).reshape(n_x, n_y, per, TR, 128), rest.reshape(n_x, n_y, per, TR, 128)]
    else:
        parts = [tc, tx, te]
        if per * cut > used:
            parts.append(jnp.zeros((n_s, per * cut - used, TR, 128), jnp.float32))
        tiles = jnp.concatenate(parts, axis=1)
        buf = tiles.reshape(n_s, n_core, n_xh, n_y, per, TR, 128)
        buf = list(jnp.transpose(buf, (1, 2, 0, 3, 4, 5, 6)).reshape(n_core, n_x, n_y, per, TR, 128))

    summed_t, sum_squares = reduce_flat(buf)
    mean_t = summed_t.reshape(per * cut, TR, 128)
    inverse = 1.0 / total
    mt = mean_t.astype(jnp.float32) * inverse
    gc = mt[: counts[0]].reshape(layers, ch_pad // TR, lanes_c, TR, 128)
    mean_c = from_tiles(gc, ch_pad, half)[:, :ch, :]
    gx = mt[counts[0] : counts[0] + counts[1]].reshape(layers, half // TR, 1, TR, 128)
    mean_x = from_tiles(gx, half, xw)
    ge = mt[counts[0] + counts[1] : used].reshape(rows_e // (TR * n_s), width // 128, TR, 128)
    mean_e = from_tiles(ge, rows_e // n_s, width)

    squares = sum_squares * (inverse * inverse)
    norm_value = jnp.sqrt(squares)
    clip_factor = jnp.minimum(1.0, 1.0 / (norm_value + 1e-06))
    wx, mx, vx = adamw_update(weight_xproj, moment_xproj, second_xproj, mean_x, clip_factor)
    wc, mc, vc = adamw_update(weight_chan, moment_chan, second_chan, mean_c, clip_factor)
    we, me, ve = adamw_update(weight_embed, moment_embed, second_embed, mean_e, clip_factor)
    bx = wx.astype(jnp.bfloat16)
    bc = wc.astype(jnp.bfloat16)
    be = we.astype(jnp.bfloat16)
    full_x = place(bx, swap_halves(bx, 0), 1)
    full_c = place(bc, swap_halves(bc, 0), 2)
    full_e = place(be, swap_halves(be, 0), 0)
    return (wx, wc, we, mx, mc, me, vx, vc, ve, full_x, full_c, full_e, jnp.reshape(norm_value, (1,)))


def solution(mesh):
    rep = mesh.shape["rep"]
    fine = Mesh(mesh.devices.reshape(rep // 16, 4, 2, 2, mesh.shape["shard"]), AXES)
    grads = ("z", "y", "xh", "core", "shard")
    placed = (
        P(grads, None, None, None),
        P(grads, None, None, None),
        P(grads, None, None),
        P(None, "shard", None),
        P(None, None, "shard"),
        P("shard", None),
        P(None, "shard", None),
        P(None, None, "shard"),
        P("shard", None),
        P(None, "shard", None),
        P(None, None, "shard"),
        P("shard", None),
    )
    return jax.shard_map(
        on_device,
        mesh=fine,
        in_specs=placed,
        out_specs=(
            P(None, "shard", None),
            P(None, None, "shard"),
            P("shard", None),
            P(None, "shard", None),
            P(None, None, "shard"),
            P("shard", None),
            P(None, "shard", None),
            P(None, None, "shard"),
            P("shard", None),
            P(),
            P(),
            P(),
            P(),
        ),
        check_vma=False,
    )
```
